128 devices in a mesh: gx: 8 (over x, core), gy: 16 (over y, z).
Axes of the slice: x: 4, y: 4, z: 4, core: 2. Of those that a mesh axis runs over, the one named last changes fastest.
Arguments:
- coeffs: bfloat16 [3072, 2, 2, 2160], P(('gx', 'gy')), may hold values from -0.00390625 to 0.00390625
- legendre: bfloat16 [3072, 2160, 128], P(('gx', 'gy')), may hold values from -6 to 6
- orders: int32 [3072], P(('gx', 'gy')), may hold values from -1 to 2159, as said below
- lat_map: int32 [256], replicated, may hold values from 0 to 255, each once
- weights: float32 [128], replicated, may hold values from 0.5 to 2
Outputs:
- grid_square: bfloat16 [256, 2, 4320], P(('gx', 'gy'))
- spectra: bfloat16 [3072, 2, 2, 2160], P(('gx', 'gy'))
The draws below stay inside these ranges and needn't reach their ends.
Inputs may be any that keep to these rules, and one draw needn't show every extreme that they name: Every order 0 to 2159 stands in exactly one slot and the other slots hold -1; in every draw the 24 slots of some device all hold orders. `lat_map`: each latitude stands in exactly one row.
All inputs are finite; a program needn't handle non-finite values.
Results may differ from the reference program's by a relative error of at most 0.012.
Values may be sent and summed in bfloat16 or wider, within the bound.
No kernel may reach another device: no remote copies, remote signals or barrier semaphores. Data moves between devices by JAX's collectives and lax.ppermute only.
A program may use at most 128 MiB of HBM per device.

```python
import math
import jax
import jax.numpy as jnp
from jax import lax

NDEG = 2160
EPOCHS = 2
NLAT = 256
NH = 128
CAP = 24
SLOTS = 3072


def draw_orders(key, part):
    first_key, second_key, third_key = jax.random.split(jax.random.fold_in(key, 7331), 3)
    rank_keys = jax.random.permutation(first_key, SLOTS).astype(jnp.int32)
    full_device = jax.random.randint(second_key, (), 0, SLOTS // CAP)
    owner = jnp.arange(SLOTS, dtype=jnp.int32) // CAP
    rank_keys = jnp.where(owner == full_device, rank_keys - SLOTS, rank_keys)
    fill_order = jnp.argsort(rank_keys, stable=True).astype(jnp.int32)
    order_values = jax.random.permutation(third_key, NDEG).astype(jnp.int32)
    result = jnp.full((SLOTS,), -1, jnp.int32)
    return result.at[fill_order[:NDEG]].set(order_values)


def steps_of(stream_key, dims, cuts, low, largest):
    def one(position, shards_of):
        heights = jax.random.uniform(jax.random.fold_in(jax.random.fold_in(stream_key, 6), position), (shards_of,), jnp.float32, low / len(cuts), largest / len(cuts))
        return jnp.repeat(jnp.exp(heights), dims[position] // shards_of).reshape((-1,) + (1,) * (len(dims) - position - 1))

    level = one(*cuts[0])
    for cut in cuts[1:]:
        level = level * one(*cut)
    return level


def normal_values(rng, dims, width, limit, cuts=(), held_as=jnp.bfloat16):
    loudness = steps_of(rng, dims, cuts, -0.22, 0.18) if cuts else 1.0
    values = jax.random.normal(rng, dims, jnp.float32) * width * loudness
    return jnp.minimum(jnp.maximum(values, -limit), limit).astype(held_as)


def setup_inputs(seed: int = 0) -> dict:
    streams_of = jax.random.split(jax.random.key(seed), 6)
    return {
        "coeffs": normal_values(streams_of[0], (SLOTS, EPOCHS, 2, NDEG), (NDEG * NDEG // 2) ** -0.5, 0.00390625, ((0, 128),)),
        "legendre": normal_values(streams_of[1], (SLOTS, NDEG, NH), 1.0, 6.0, ((0, 128),)),
        "orders": draw_orders(jax.random.fold_in(streams_of[5], 71), 0),
        "lat_map": jax.random.permutation(streams_of[3], NLAT).astype(jnp.int32),
        "weights": jnp.clip(jnp.exp(jax.random.uniform(streams_of[4], (NH,), jnp.float32, math.log(0.5), math.log(2.0))), 0.5, 2.0),
    }


def slot_masks(orders, deg_count):
    degrees = jnp.arange(deg_count, dtype=jnp.int32)
    usable = (orders[:, None] >= 0) & (degrees[None, :] >= orders[:, None])
    even_pair = (degrees[None, :] + orders[:, None]) % 2 == 0
    return usable, even_pair


def reference(coeffs, legendre, orders, lat_map, weights):
    deg_count = legendre.shape[1]
    half_lats = legendre.shape[2]
    lon_count = 2 * deg_count
    usable, even_pair = slot_masks(orders, deg_count)

    def synth_slot(packed):
        spectrum, legendre_row, usable_row, even_row = packed
        masked = jnp.where(usable_row, spectrum.astype(jnp.float32), jnp.float32(0.0))
        signed = jnp.where(even_row, masked, -masked)
        table_wide = legendre_row.astype(jnp.float32)
        northern = jnp.einsum("ecl,lk->eck", masked, table_wide)
        southern = jnp.einsum("ecl,lk->eck", signed, table_wide)
        return jnp.concatenate([northern, southern[..., ::-1]], axis=-1).astype(jnp.bfloat16)

    synthesized = lax.map(synth_slot, (coeffs, legendre, usable, even_pair))
    synthesized = lax.optimization_barrier(synthesized)
    target = jnp.where(orders >= 0, orders, deg_count).astype(jnp.int32)
    dense_orders = jnp.zeros((deg_count,) + synthesized.shape[1:], jnp.float32)
    dense_orders = dense_orders.at[target].set(synthesized.astype(jnp.float32), mode="drop")
    cos_part = jnp.transpose(dense_orders[:, :, 0, :], (2, 1, 0))
    sin_part = jnp.transpose(dense_orders[:, :, 1, :], (2, 1, 0))
    spectrum_all = jnp.pad(cos_part - 1j * sin_part, ((0, 0), (0, 0), (0, lon_count - deg_count)))
    grid_field = lon_count * jnp.real(jnp.fft.ifft(spectrum_all, axis=-1))
    squared = (grid_field * grid_field).astype(jnp.bfloat16)
    squared = lax.optimization_barrier(squared)
    grid_square = squared[lat_map]
    frequency = jnp.fft.fft(squared.astype(jnp.float32), axis=-1)[..., :deg_count]
    scaling = jnp.where(jnp.arange(deg_count) == 0, 1.0, 2.0).astype(jnp.float32) / lon_count
    fourier_cos = scaling * jnp.real(frequency)
    fourier_sin = -scaling * jnp.imag(frequency)
    fourier_all = jnp.transpose(jnp.stack([fourier_cos, fourier_sin], axis=2), (3, 1, 2, 0))
    slot_fourier = fourier_all[jnp.maximum(orders, 0)]

    def analyze_slot(packed):
        values, legendre_row, usable_row, even_row = packed
        northern = values[..., :half_lats]
        southern = values[..., half_lats:][..., ::-1]
        sym_part = ((northern + southern) * weights).astype(jnp.bfloat16)
        anti_part = ((northern - southern) * weights).astype(jnp.bfloat16)
        sym_part, anti_part = lax.optimization_barrier((sym_part, anti_part))
        table_wide = legendre_row.astype(jnp.float32)
        even_out = jnp.einsum("eck,lk->ecl", sym_part.astype(jnp.float32), table_wide)
        odd_out = jnp.einsum("eck,lk->ecl", anti_part.astype(jnp.float32), table_wide)
        chosen = jnp.where(even_row, even_out, odd_out)
        return jnp.where(usable_row, chosen, jnp.float32(0.0)).astype(jnp.bfloat16)

    spectra = lax.map(analyze_slot, (slot_fourier, legendre, usable, even_pair))
    return grid_square, spectra
```

```python
import math

import jax
import jax.numpy as jnp
from jax import lax
from jax.sharding import PartitionSpec as P

ORDER_BASE = 64


def slot_masks(orders, deg_count):
    degrees = jnp.arange(deg_count, dtype=jnp.int32)
    usable = (orders[:, None] >= 0) & (degrees[None, :] >= orders[:, None])
    even_pair = (degrees[None, :] + orders[:, None]) % 2 == 0
    return (usable, even_pair)


def inner_length(lon_count):
    best = 1
    for factor in range(1, math.isqrt(lon_count) + 1):
        if lon_count % factor == 0:
            best = factor
    return best


def phase_tables(order_vals, stride, count, lon_count):
    positions = jnp.arange(count, dtype=jnp.int32) * stride
    phase_int = positions[:, None] * order_vals[None, :] % lon_count
    angles = phase_int.astype(jnp.float32) * jnp.float32(2.0 * math.pi / lon_count)
    filled = order_vals[None, :] >= 0
    cosine = jnp.where(filled, jnp.cos(angles), jnp.float32(0.0))
    sine_tab = jnp.where(filled, jnp.sin(angles), jnp.float32(0.0))
    return (cosine, sine_tab)


def one_hot_rows(lat_map, lat_rows):
    return (lat_map[None, :] == jnp.arange(lat_rows, dtype=jnp.int32)[:, None]).astype(jnp.bfloat16)


def transform_rows(coef, order_vals, lon_count):
    high = lax.Precision.HIGH
    inner_len = inner_length(lon_count)
    outer_len = lon_count // inner_len
    cos_outer, sin_outer = phase_tables(order_vals, inner_len, outer_len, lon_count)
    cos_inner, sin_inner = phase_tables(order_vals, 1, inner_len, lon_count)
    coef_cos = coef[:, 0, :]
    coef_sin = coef[:, 1, :]
    y_real = coef_cos.T[:, None, :] * cos_outer[None] + coef_sin.T[:, None, :] * sin_outer[None]
    y_imag = coef_cos.T[:, None, :] * sin_outer[None] - coef_sin.T[:, None, :] * cos_outer[None]
    y_both = jnp.concatenate([y_real, y_imag], axis=-1)
    inner_both = jnp.concatenate([cos_inner, -sin_inner], axis=-1)
    grid_field = jnp.einsum("ras,bs->rab", y_both, inner_both, precision=high)
    signals = grid_field.shape[0]
    squared = (grid_field * grid_field).astype(jnp.bfloat16)
    sq_wide = squared.astype(jnp.float32)
    g_real = jnp.einsum("rab,bs->ras", sq_wide, cos_inner, precision=high)
    g_imag = -jnp.einsum("rab,bs->ras", sq_wide, sin_inner, precision=high)
    four_cos = jnp.sum(g_real * cos_outer[None] + g_imag * sin_outer[None], axis=1)
    four_sin = jnp.sum(g_real * sin_outer[None] - g_imag * cos_outer[None], axis=1)
    scaling = jnp.where(order_vals == 0, 1.0, 2.0).astype(jnp.float32) / lon_count
    fourier = jnp.stack([four_cos, four_sin], axis=1) * scaling[None, None, :]
    return squared.reshape(signals, lon_count), fourier


def shards(coeffs, legendre, orders, lat_map, weights):
    slot_cap = coeffs.shape[0]
    epoch_count = coeffs.shape[1]
    deg_count = legendre.shape[1]
    half_lats = legendre.shape[2]
    lon_count = 2 * deg_count
    lat_rows = lat_map.shape[0]
    devices = lax.axis_size(("gx", "gy"))
    rows_each = lat_rows // devices
    usable, even_pair = slot_masks(orders, deg_count)

    zero_half = jnp.zeros((), jnp.bfloat16)
    masked = jnp.where(usable[:, None, None, :], coeffs, zero_half)
    signed = jnp.where(even_pair[:, None, None, :], masked, -masked)
    stacked = jnp.concatenate([masked, signed], axis=1).reshape(slot_cap, 2 * epoch_count * 2, deg_count)
    synth = jnp.einsum("sxl,slk->sxk", stacked, legendre, preferred_element_type=jnp.float32)
    synth = synth.astype(jnp.bfloat16).reshape(slot_cap, 2, epoch_count * 2, half_lats)
    full_lats = jnp.concatenate([synth[:, 0], synth[:, 1, :, ::-1]], axis=-1)

    onehot = one_hot_rows(lat_map, lat_rows)
    permuted = jnp.einsum(
        "sxk,kr->sxr", full_lats, onehot, preferred_element_type=jnp.float32
    ).astype(jnp.bfloat16)
    sends = permuted.reshape(slot_cap, epoch_count * 2, devices, rows_each)
    sends = jnp.transpose(sends, (2, 0, 1, 3)).reshape(devices, slot_cap, epoch_count * 2 * rows_each)
    coded = orders + 1
    order_code = jnp.stack([coded // ORDER_BASE, coded % ORDER_BASE], axis=-1).astype(jnp.bfloat16)
    order_code = jnp.broadcast_to(order_code[None], (devices, slot_cap, 2))
    payload = jnp.concatenate([sends, order_code], axis=-1)
    got = lax.all_to_all(payload, ("gx", "gy"), 0, 0, tiled=True)
    got = got.reshape(devices * slot_cap, -1)
    code = got[:, -2:].astype(jnp.int32)
    all_orders = code[:, 0] * ORDER_BASE + code[:, 1] - 1
    received = got[:, :-2].reshape(devices * slot_cap, epoch_count, 2, rows_each)
    coef = jnp.transpose(received, (0, 2, 3, 1)).reshape(devices * slot_cap, 2, rows_each * epoch_count)
    squared, fourier = transform_rows(coef.astype(jnp.float32), all_orders, lon_count)
    grid_rows = squared.reshape(rows_each, epoch_count, lon_count)

    back = jnp.transpose(fourier, (2, 1, 0)).astype(jnp.bfloat16).reshape(devices, slot_cap, 2, rows_each, epoch_count)
    back = lax.all_to_all(back, ("gx", "gy"), 0, 0, tiled=True)
    returned = jnp.transpose(back, (1, 4, 2, 0, 3)).reshape(slot_cap, epoch_count * 2, lat_rows)
    natural = jnp.einsum(
        "sxr,kr->sxk", returned, onehot, preferred_element_type=jnp.float32
    )
    northern = natural[..., :half_lats]
    southern = natural[..., half_lats:][..., ::-1]
    sym_part = ((northern + southern) * weights).astype(jnp.bfloat16)
    anti_part = ((northern - southern) * weights).astype(jnp.bfloat16)
    both = jnp.concatenate([sym_part, anti_part], axis=1)
    out = jnp.einsum("sxk,slk->sxl", both, legendre, preferred_element_type=jnp.float32)
    out = out.reshape(slot_cap, 2, epoch_count, 2, deg_count)
    chosen = jnp.where(even_pair[:, None, None, :], out[:, 0], out[:, 1])
    spectra = jnp.where(usable[:, None, None, :], chosen, jnp.float32(0.0)).astype(jnp.bfloat16)
    return (grid_rows, spectra)


def solution(mesh):
    placed = (
        P(("gx", "gy"), None, None, None),
        P(("gx", "gy"), None, None),
        P(("gx", "gy")),
        P(),
        P(),
    )
    return jax.shard_map(
        shards,
        mesh=mesh,
        in_specs=placed,
        out_specs=(P(("gx", "gy"), None, None), P(("gx", "gy"), None, None, None)),
        check_vma=False,
    )
```

```python
import math

import jax
import jax.numpy as jnp
from jax import lax
from jax.experimental import pallas as pl
from jax.experimental.pallas import tpu as pltpu
from jax.sharding import PartitionSpec as P

ORDER_BASE = 64

SLOTS_PER_STEP = 6


def _masks(order, deg_count):
    degrees = lax.broadcasted_iota(jnp.int32, (1, deg_count), 1)
    usable = (degrees >= order) & (order >= 0)
    even = ((degrees + order) & 1) == 0
    return usable, even


def _synth_kernel(orders_ref, coef_ref, leg_ref, out_ref):
    step = pl.program_id(0)
    block, epochs, _, deg_count = coef_ref.shape
    zero = jnp.zeros((), coef_ref.dtype)
    for i in range(block):
        order = orders_ref[step * block + i]
        usable, even = _masks(order, deg_count)
        rows = jnp.concatenate([coef_ref[i, e] for e in range(epochs)], axis=0)
        masked = jnp.where(usable, rows, zero)
        signed = jnp.where(even, masked, -masked)
        lhs = jnp.concatenate([masked, signed], axis=0)
        out_ref[i] = jnp.dot(lhs, leg_ref[i], preferred_element_type=jnp.float32).astype(out_ref.dtype)


def synthesize(coeffs, legendre, orders):
    slot_cap, epochs, parts, deg_count = coeffs.shape
    half_lats = legendre.shape[2]
    block = SLOTS_PER_STEP
    rows = 2 * epochs * parts
    grid_spec = pltpu.PrefetchScalarGridSpec(
        num_scalar_prefetch=1,
        grid=(slot_cap // block,),
        in_specs=[
            pl.BlockSpec((block, epochs, parts, deg_count), lambda g, o: (g, 0, 0, 0)),
            pl.BlockSpec((block, deg_count, half_lats), lambda g, o: (g, 0, 0)),
        ],
        out_specs=pl.BlockSpec((block, rows, half_lats), lambda g, o: (g, 0, 0)),
    )
    return pl.pallas_call(
        _synth_kernel,
        grid_spec=grid_spec,
        out_shape=jax.ShapeDtypeStruct((slot_cap, rows, half_lats), jnp.bfloat16),
        compiler_params=pltpu.CompilerParams(dimension_semantics=("arbitrary",)),
        cost_estimate=pl.CostEstimate(
            flops=2 * slot_cap * rows * deg_count * half_lats,
            bytes_accessed=legendre.size * 2 + coeffs.size * 2 + slot_cap * rows * half_lats * 2,
            transcendentals=0,
        ),
    )(orders, coeffs, legendre)


def _analysis_kernel(orders_ref, both_ref, leg_ref, out_ref):
    step = pl.program_id(0)
    block, epochs, parts, deg_count = out_ref.shape
    half = epochs * parts
    for i in range(block):
        order = orders_ref[step * block + i]
        usable, even = _masks(order, deg_count)
        res = lax.dot_general(
            both_ref[i], leg_ref[i], (((1,), (1,)), ((), ())), preferred_element_type=jnp.float32
        )
        chosen = jnp.where(even, res[:half], res[half:])
        chosen = jnp.where(usable, chosen, jnp.float32(0.0)).astype(out_ref.dtype)
        for e in range(epochs):
            out_ref[i, e] = chosen[e * parts:(e + 1) * parts]


def analyze(both, legendre, orders, epochs, parts):
    slot_cap, rows, half_lats = both.shape
    deg_count = legendre.shape[1]
    block = SLOTS_PER_STEP
    grid_spec = pltpu.PrefetchScalarGridSpec(
        num_scalar_prefetch=1,
        grid=(slot_cap // block,),
        in_specs=[
            pl.BlockSpec((block, rows, half_lats), lambda g, o: (g, 0, 0)),
            pl.BlockSpec((block, deg_count, half_lats), lambda g, o: (g, 0, 0)),
        ],
        out_specs=pl.BlockSpec((block, epochs, parts, deg_count), lambda g, o: (g, 0, 0, 0)),
    )
    return pl.pallas_call(
        _analysis_kernel,
        grid_spec=grid_spec,
        out_shape=jax.ShapeDtypeStruct((slot_cap, epochs, parts, deg_count), jnp.bfloat16),
        compiler_params=pltpu.CompilerParams(dimension_semantics=("arbitrary",)),
        cost_estimate=pl.CostEstimate(
            flops=2 * slot_cap * rows * deg_count * half_lats,
            bytes_accessed=legendre.size * 2 + both.size * 2 + slot_cap * epochs * parts * deg_count * 2,
            transcendentals=0,
        ),
    )(orders, both, legendre)


def inner_length(lon_count):
    best = 1
    for factor in range(1, math.isqrt(lon_count) + 1):
        if lon_count % factor == 0:
            best = factor
    return best


def phase_tables(order_vals, stride, count, lon_count):
    positions = jnp.arange(count, dtype=jnp.int32) * stride
    phase_int = positions[:, None] * order_vals[None, :] % lon_count
    angles = phase_int.astype(jnp.float32) * jnp.float32(2.0 * math.pi / lon_count)
    filled = order_vals[None, :] >= 0
    cosine = jnp.where(filled, jnp.cos(angles), jnp.float32(0.0))
    sine_tab = jnp.where(filled, jnp.sin(angles), jnp.float32(0.0))
    return (cosine, sine_tab)


def one_hot_rows(lat_map, lat_rows):
    return (lat_map[None, :] == jnp.arange(lat_rows, dtype=jnp.int32)[:, None]).astype(jnp.bfloat16)


def transform_rows(coef, order_vals, lon_count):
    high = lax.Precision.HIGH
    inner_len = inner_length(lon_count)
    outer_len = lon_count // inner_len
    cos_outer, sin_outer = phase_tables(order_vals, inner_len, outer_len, lon_count)
    cos_inner, sin_inner = phase_tables(order_vals, 1, inner_len, lon_count)
    coef_cos = coef[:, 0, :]
    coef_sin = coef[:, 1, :]
    y_real = coef_cos.T[:, None, :] * cos_outer[None] + coef_sin.T[:, None, :] * sin_outer[None]
    y_imag = coef_cos.T[:, None, :] * sin_outer[None] - coef_sin.T[:, None, :] * cos_outer[None]
    y_both = jnp.concatenate([y_real, y_imag], axis=-1)
    inner_both = jnp.concatenate([cos_inner, -sin_inner], axis=-1)
    grid_field = jnp.einsum("ras,bs->rab", y_both, inner_both, precision=high)
    signals = grid_field.shape[0]
    squared = (grid_field * grid_field).astype(jnp.bfloat16)
    sq_wide = squared.astype(jnp.float32)
    g_real = jnp.einsum("rab,bs->ras", sq_wide, cos_inner, precision=high)
    g_imag = -jnp.einsum("rab,bs->ras", sq_wide, sin_inner, precision=high)
    four_cos = jnp.sum(g_real * cos_outer[None] + g_imag * sin_outer[None], axis=1)
    four_sin = jnp.sum(g_real * sin_outer[None] - g_imag * cos_outer[None], axis=1)
    scaling = jnp.where(order_vals == 0, 1.0, 2.0).astype(jnp.float32) / lon_count
    fourier = jnp.stack([four_cos, four_sin], axis=1) * scaling[None, None, :]
    return squared.reshape(signals, lon_count), fourier


def shards(coeffs, legendre, orders, lat_map, weights):
    slot_cap = coeffs.shape[0]
    epoch_count = coeffs.shape[1]
    deg_count = legendre.shape[1]
    half_lats = legendre.shape[2]
    lon_count = 2 * deg_count
    lat_rows = lat_map.shape[0]
    devices = lax.axis_size(("gx", "gy"))
    rows_each = lat_rows // devices

    synth = synthesize(coeffs, legendre, orders).reshape(slot_cap, 2, epoch_count * 2, half_lats)
    full_lats = jnp.concatenate([synth[:, 0], synth[:, 1, :, ::-1]], axis=-1)

    onehot = one_hot_rows(lat_map, lat_rows)
    permuted = jnp.einsum(
        "sxk,kr->sxr", full_lats, onehot, preferred_element_type=jnp.float32
    ).astype(jnp.bfloat16)
    sends = permuted.reshape(slot_cap, epoch_count * 2, devices, rows_each)
    sends = jnp.transpose(sends, (2, 0, 1, 3)).reshape(devices, slot_cap, epoch_count * 2 * rows_each)
    coded = orders + 1
    order_code = jnp.stack([coded // ORDER_BASE, coded % ORDER_BASE], axis=-1).astype(jnp.bfloat16)
    order_code = jnp.broadcast_to(order_code[None], (devices, slot_cap, 2))
    payload = jnp.concatenate([sends, order_code], axis=-1)
    got = lax.all_to_all(payload, ("gx", "gy"), 0, 0, tiled=True)
    got = got.reshape(devices * slot_cap, -1)
    code = got[:, -2:].astype(jnp.int32)
    all_orders = code[:, 0] * ORDER_BASE + code[:, 1] - 1
    received = got[:, :-2].reshape(devices * slot_cap, epoch_count, 2, rows_each)
    coef = jnp.transpose(received, (0, 2, 3, 1)).reshape(devices * slot_cap, 2, rows_each * epoch_count)
    squared, fourier = transform_rows(coef.astype(jnp.float32), all_orders, lon_count)
    grid_rows = squared.reshape(rows_each, epoch_count, lon_count)

    back = jnp.transpose(fourier, (2, 1, 0)).astype(jnp.bfloat16).reshape(devices, slot_cap, 2, rows_each, epoch_count)
    back = lax.all_to_all(back, ("gx", "gy"), 0, 0, tiled=True)
    returned = jnp.transpose(back, (1, 4, 2, 0, 3)).reshape(slot_cap, epoch_count * 2, lat_rows)
    natural = jnp.einsum(
        "sxr,kr->sxk", returned, onehot, preferred_element_type=jnp.float32
    )
    northern = natural[..., :half_lats]
    southern = natural[..., half_lats:][..., ::-1]
    sym_part = ((northern + southern) * weights).astype(jnp.bfloat16)
    anti_part = ((northern - southern) * weights).astype(jnp.bfloat16)
    both = jnp.concatenate([sym_part, anti_part], axis=1)
    spectra = analyze(both, legendre, orders, epoch_count, 2)
    return (grid_rows, spectra)


def solution(mesh):
    placed = (
        P(("gx", "gy"), None, None, None),
        P(("gx", "gy"), None, None),
        P(("gx", "gy")),
        P(),
        P(),
    )
    return jax.shard_map(
        shards,
        mesh=mesh,
        in_specs=placed,
        out_specs=(P(("gx", "gy"), None, None), P(("gx", "gy"), None, None, None)),
        check_vma=False,
    )
```

```python
import math

import jax
import jax.numpy as jnp
from jax import lax
from jax.experimental import pallas as pl
from jax.experimental.pallas import tpu as pltpu
from jax.sharding import PartitionSpec as P

ORDER_BASE = 64

SLOTS_PER_STEP = 6


def _masks(order, deg_count):
    degrees = lax.broadcasted_iota(jnp.int32, (1, deg_count), 1)
    usable = (degrees >= order) & (order >= 0)
    even = ((degrees + order) & 1) == 0
    return usable, even


def _synth_kernel(orders_ref, coef_ref, leg_ref, out_ref):
    step = pl.program_id(0)
    block, epochs, _, deg_count = coef_ref.shape
    zero = jnp.zeros((), coef_ref.dtype)
    for i in range(block):
        order = orders_ref[step * block + i]
        usable, even = _masks(order, deg_count)
        rows = jnp.concatenate([coef_ref[i, e] for e in range(epochs)], axis=0)
        masked = jnp.where(usable, rows, zero)
        signed = jnp.where(even, masked, -masked)
        lhs = jnp.concatenate([masked, signed], axis=0)
        out_ref[i] = jnp.dot(lhs, leg_ref[i], preferred_element_type=jnp.float32).astype(out_ref.dtype)


def synthesize(coeffs, legendre, orders):
    slot_cap, epochs, parts, deg_count = coeffs.shape
    half_lats = legendre.shape[2]
    block = SLOTS_PER_STEP
    rows = 2 * epochs * parts
    grid_spec = pltpu.PrefetchScalarGridSpec(
        num_scalar_prefetch=1,
        grid=(slot_cap // block,),
        in_specs=[
            pl.BlockSpec((block, epochs, parts, deg_count), lambda g, o: (g, 0, 0, 0)),
            pl.BlockSpec((block, deg_count, half_lats), lambda g, o: (g, 0, 0)),
        ],
        out_specs=pl.BlockSpec((block, rows, half_lats), lambda g, o: (g, 0, 0)),
    )
    return pl.pallas_call(
        _synth_kernel,
        grid_spec=grid_spec,
        out_shape=jax.ShapeDtypeStruct((slot_cap, rows, half_lats), jnp.bfloat16),
        compiler_params=pltpu.CompilerParams(dimension_semantics=("arbitrary",)),
        cost_estimate=pl.CostEstimate(
            flops=2 * slot_cap * rows * deg_count * half_lats,
            bytes_accessed=legendre.size * 2 + coeffs.size * 2 + slot_cap * rows * half_lats * 2,
            transcendentals=0,
        ),
    )(orders, coeffs, legendre)


def _analysis_kernel(orders_ref, both_ref, leg_ref, out_ref):
    step = pl.program_id(0)
    block, epochs, parts, deg_count = out_ref.shape
    half = epochs * parts
    for i in range(block):
        order = orders_ref[step * block + i]
        usable, even = _masks(order, deg_count)
        res = lax.dot_general(
            both_ref[i], leg_ref[i], (((1,), (1,)), ((), ())), preferred_element_type=jnp.float32
        )
        chosen = jnp.where(even, res[:half], res[half:])
        chosen = jnp.where(usable, chosen, jnp.float32(0.0)).astype(out_ref.dtype)
        for e in range(epochs):
            out_ref[i, e] = chosen[e * parts:(e + 1) * parts]


def analyze(both, legendre, orders, epochs, parts):
    slot_cap, rows, half_lats = both.shape
    deg_count = legendre.shape[1]
    block = SLOTS_PER_STEP
    grid_spec = pltpu.PrefetchScalarGridSpec(
        num_scalar_prefetch=1,
        grid=(slot_cap // block,),
        in_specs=[
            pl.BlockSpec((block, rows, half_lats), lambda g, o: (g, 0, 0)),
            pl.BlockSpec((block, deg_count, half_lats), lambda g, o: (g, 0, 0)),
        ],
        out_specs=pl.BlockSpec((block, epochs, parts, deg_count), lambda g, o: (g, 0, 0, 0)),
    )
    return pl.pallas_call(
        _analysis_kernel,
        grid_spec=grid_spec,
        out_shape=jax.ShapeDtypeStruct((slot_cap, epochs, parts, deg_count), jnp.bfloat16),
        compiler_params=pltpu.CompilerParams(dimension_semantics=("arbitrary",)),
        cost_estimate=pl.CostEstimate(
            flops=2 * slot_cap * rows * deg_count * half_lats,
            bytes_accessed=legendre.size * 2 + both.size * 2 + slot_cap * epochs * parts * deg_count * 2,
            transcendentals=0,
        ),
    )(orders, both, legendre)


def inner_length(lon_count):
    best = 1
    for factor in range(1, math.isqrt(lon_count) + 1):
        if lon_count % factor == 0:
            best = factor
    return best


def one_hot_rows(lat_map, lat_rows):
    return (lat_map[None, :] == jnp.arange(lat_rows, dtype=jnp.int32)[:, None]).astype(jnp.bfloat16)


def angle(numer, denom):
    return jnp.float32(2.0 * math.pi) * (numer % denom).astype(jnp.float32) / jnp.float32(denom)


def transform_dense(dense, lon_count):
    highest = lax.Precision.HIGHEST
    deg_count, _, signals = dense.shape
    inner = inner_length(lon_count)
    outer = lon_count // inner
    blocks = deg_count // outer
    a_idx = jnp.arange(outer, dtype=jnp.int32)
    b_idx = jnp.arange(inner, dtype=jnp.int32)
    c_idx = jnp.arange(blocks, dtype=jnp.int32)
    w1 = angle(b_idx[:, None] * c_idx[None, :], inner)
    w1c, w1s = jnp.cos(w1), jnp.sin(w1)
    tw = angle(b_idx[:, None] * a_idx[None, :], lon_count)
    twc, tws = jnp.cos(tw)[:, :, None], jnp.sin(tw)[:, :, None]
    w2 = angle(a_idx[:, None] * a_idx[None, :], outer)
    w2c, w2s = jnp.cos(w2), jnp.sin(w2)
    x_re = dense[:, 0, :].reshape(blocks, outer, signals)
    x_im = -dense[:, 1, :].reshape(blocks, outer, signals)

    def mm(spec, left, right):
        return jnp.einsum(spec, left, right, precision=highest)

    y_re = mm("bc,cdq->bdq", w1c, x_re) - mm("bc,cdq->bdq", w1s, x_im)
    y_im = mm("bc,cdq->bdq", w1c, x_im) + mm("bc,cdq->bdq", w1s, x_re)
    t_re = y_re * twc - y_im * tws
    t_im = y_re * tws + y_im * twc
    field = mm("ad,bdq->abq", w2c, t_re) - mm("ad,bdq->abq", w2s, t_im)
    squared = (field * field).astype(jnp.bfloat16)
    sq = squared.astype(jnp.float32)
    z_re = mm("da,abq->bdq", w2c, sq)
    z_im = -mm("da,abq->bdq", w2s, sq)
    u_re = z_re * twc + z_im * tws
    u_im = z_im * twc - z_re * tws
    f_re = mm("bc,bdq->cdq", w1c, u_re) + mm("bc,bdq->cdq", w1s, u_im)
    f_im = mm("bc,bdq->cdq", w1c, u_im) - mm("bc,bdq->cdq", w1s, u_re)
    m_idx = jnp.arange(deg_count, dtype=jnp.int32)
    scaling = jnp.where(m_idx == 0, 1.0, 2.0).astype(jnp.float32)[:, None] / lon_count
    four_cos = f_re.reshape(deg_count, signals) * scaling
    four_sin = -f_im.reshape(deg_count, signals) * scaling
    grid = jnp.transpose(squared, (2, 0, 1)).reshape(signals, lon_count)
    return grid, jnp.stack([four_cos, four_sin], axis=1)


def shards(coeffs, legendre, orders, lat_map, weights):
    slot_cap = coeffs.shape[0]
    epoch_count = coeffs.shape[1]
    deg_count = legendre.shape[1]
    half_lats = legendre.shape[2]
    lon_count = 2 * deg_count
    lat_rows = lat_map.shape[0]
    devices = lax.axis_size(("gx", "gy"))
    rows_each = lat_rows // devices

    synth = synthesize(coeffs, legendre, orders).reshape(slot_cap, 2, epoch_count * 2, half_lats)
    full_lats = jnp.concatenate([synth[:, 0], synth[:, 1, :, ::-1]], axis=-1)

    onehot = one_hot_rows(lat_map, lat_rows)
    permuted = jnp.einsum(
        "sxk,kr->sxr", full_lats, onehot, preferred_element_type=jnp.float32
    ).astype(jnp.bfloat16)
    sends = permuted.reshape(slot_cap, epoch_count * 2, devices, rows_each)
    sends = jnp.transpose(sends, (2, 0, 1, 3)).reshape(devices, slot_cap, epoch_count * 2 * rows_each)
    coded = orders + 1
    order_code = jnp.stack([coded // ORDER_BASE, coded % ORDER_BASE], axis=-1).astype(jnp.bfloat16)
    order_code = jnp.broadcast_to(order_code[None], (devices, slot_cap, 2))
    payload = jnp.concatenate([sends, order_code], axis=-1)
    got = lax.all_to_all(payload, ("gx", "gy"), 0, 0, tiled=True)
    got = got.reshape(devices * slot_cap, -1)
    code = got[:, -2:].astype(jnp.int32)
    all_orders = code[:, 0] * ORDER_BASE + code[:, 1] - 1
    data = got[:, :-2]
    dense_map = (all_orders[:, None] == jnp.arange(deg_count, dtype=jnp.int32)[None, :]).astype(jnp.bfloat16)
    dense = jnp.einsum("sm,sr->mr", dense_map, data, preferred_element_type=jnp.float32)
    dense = dense.reshape(deg_count, epoch_count, 2, rows_each)
    dense = jnp.transpose(dense, (0, 2, 1, 3)).reshape(deg_count, 2, epoch_count * rows_each)
    grid, fourier = transform_dense(dense, lon_count)
    grid_rows = jnp.transpose(grid.reshape(epoch_count, rows_each, lon_count), (1, 0, 2))

    fourier = fourier.astype(jnp.bfloat16).reshape(deg_count, 2, epoch_count, rows_each)
    fourier = jnp.transpose(fourier, (0, 2, 1, 3)).reshape(deg_count, -1)
    by_slot = jnp.einsum("sm,mr->sr", dense_map, fourier, preferred_element_type=jnp.float32)
    back = by_slot.astype(jnp.bfloat16).reshape(devices, slot_cap, epoch_count, 2, rows_each)
    back = lax.all_to_all(back, ("gx", "gy"), 0, 0, tiled=True)
    returned = jnp.transpose(back, (1, 2, 3, 0, 4)).reshape(slot_cap, epoch_count * 2, lat_rows)
    natural = jnp.einsum(
        "sxr,kr->sxk", returned, onehot, preferred_element_type=jnp.float32
    )
    northern = natural[..., :half_lats]
    southern = natural[..., half_lats:][..., ::-1]
    sym_part = ((northern + southern) * weights).astype(jnp.bfloat16)
    anti_part = ((northern - southern) * weights).astype(jnp.bfloat16)
    both = jnp.concatenate([sym_part, anti_part], axis=1)
    spectra = analyze(both, legendre, orders, epoch_count, 2)
    return (grid_rows, spectra)


def solution(mesh):
    placed = (
        P(("gx", "gy"), None, None, None),
        P(("gx", "gy"), None, None),
        P(("gx", "gy")),
        P(),
        P(),
    )
    return jax.shard_map(
        shards,
        mesh=mesh,
        in_specs=placed,
        out_specs=(P(("gx", "gy"), None, None), P(("gx", "gy"), None, None, None)),
        check_vma=False,
    )
```

```python
import math

import jax
import jax.numpy as jnp
from jax import lax
from jax.experimental import pallas as pl
from jax.experimental.pallas import tpu as pltpu
from jax.sharding import PartitionSpec as P


SLOTS_PER_STEP = 6


def _masks(order, deg_count):
    degrees = lax.broadcasted_iota(jnp.int32, (1, deg_count), 1)
    usable = (degrees >= order) & (order >= 0)
    even = ((degrees + order) & 1) == 0
    return usable, even


def _synth_kernel(orders_ref, coef_ref, leg_ref, out_ref):
    step = pl.program_id(0)
    block, epochs, _, deg_count = coef_ref.shape
    zero = jnp.zeros((), coef_ref.dtype)
    for i in range(block):
        order = orders_ref[step * block + i]
        usable, even = _masks(order, deg_count)
        rows = jnp.concatenate([coef_ref[i, e] for e in range(epochs)], axis=0)
        masked = jnp.where(usable, rows, zero)
        signed = jnp.where(even, masked, -masked)
        lhs = jnp.concatenate([masked, signed], axis=0)
        out_ref[i] = jnp.dot(lhs, leg_ref[i], preferred_element_type=jnp.float32).astype(out_ref.dtype)


def synthesize(coeffs, legendre, orders):
    slot_cap, epochs, parts, deg_count = coeffs.shape
    half_lats = legendre.shape[2]
    block = SLOTS_PER_STEP
    rows = 2 * epochs * parts
    grid_spec = pltpu.PrefetchScalarGridSpec(
        num_scalar_prefetch=1,
        grid=(slot_cap // block,),
        in_specs=[
            pl.BlockSpec((block, epochs, parts, deg_count), lambda g, o: (g, 0, 0, 0)),
            pl.BlockSpec((block, deg_count, half_lats), lambda g, o: (g, 0, 0)),
        ],
        out_specs=pl.BlockSpec((block, rows, half_lats), lambda g, o: (g, 0, 0)),
    )
    return pl.pallas_call(
        _synth_kernel,
        grid_spec=grid_spec,
        out_shape=jax.ShapeDtypeStruct((slot_cap, rows, half_lats), jnp.bfloat16),
        compiler_params=pltpu.CompilerParams(dimension_semantics=("arbitrary",)),
        cost_estimate=pl.CostEstimate(
            flops=2 * slot_cap * rows * deg_count * half_lats,
            bytes_accessed=legendre.size * 2 + coeffs.size * 2 + slot_cap * rows * half_lats * 2,
            transcendentals=0,
        ),
    )(orders, coeffs, legendre)


def _analysis_kernel(orders_ref, both_ref, leg_ref, out_ref):
    step = pl.program_id(0)
    block, epochs, parts, deg_count = out_ref.shape
    half = epochs * parts
    for i in range(block):
        order = orders_ref[step * block + i]
        usable, even = _masks(order, deg_count)
        res = lax.dot_general(
            both_ref[i], leg_ref[i], (((1,), (1,)), ((), ())), preferred_element_type=jnp.float32
        )
        chosen = jnp.where(even, res[:half], res[half:])
        chosen = jnp.where(usable, chosen, jnp.float32(0.0)).astype(out_ref.dtype)
        for e in range(epochs):
            out_ref[i, e] = chosen[e * parts:(e + 1) * parts]


def analyze(both, legendre, orders, epochs, parts):
    slot_cap, rows, half_lats = both.shape
    deg_count = legendre.shape[1]
    block = SLOTS_PER_STEP
    grid_spec = pltpu.PrefetchScalarGridSpec(
        num_scalar_prefetch=1,
        grid=(slot_cap // block,),
        in_specs=[
            pl.BlockSpec((block, rows, half_lats), lambda g, o: (g, 0, 0)),
            pl.BlockSpec((block, deg_count, half_lats), lambda g, o: (g, 0, 0)),
        ],
        out_specs=pl.BlockSpec((block, epochs, parts, deg_count), lambda g, o: (g, 0, 0, 0)),
    )
    return pl.pallas_call(
        _analysis_kernel,
        grid_spec=grid_spec,
        out_shape=jax.ShapeDtypeStruct((slot_cap, epochs, parts, deg_count), jnp.bfloat16),
        compiler_params=pltpu.CompilerParams(dimension_semantics=("arbitrary",)),
        cost_estimate=pl.CostEstimate(
            flops=2 * slot_cap * rows * deg_count * half_lats,
            bytes_accessed=legendre.size * 2 + both.size * 2 + slot_cap * epochs * parts * deg_count * 2,
            transcendentals=0,
        ),
    )(orders, both, legendre)


def inner_length(lon_count):
    best = 1
    for factor in range(1, math.isqrt(lon_count) + 1):
        if lon_count % factor == 0:
            best = factor
    return best


def one_hot_rows(lat_map, lat_rows):
    return (lat_map[None, :] == jnp.arange(lat_rows, dtype=jnp.int32)[:, None]).astype(jnp.bfloat16)


def angle(numer, denom):
    return jnp.float32(2.0 * math.pi) * (numer % denom).astype(jnp.float32) / jnp.float32(denom)


def transform_blocks(x_parts, lon_count):
    highest = lax.Precision.HIGHEST
    _, outer, blocks, signals = x_parts.shape
    inner = lon_count // outer
    a_idx = jnp.arange(outer, dtype=jnp.int32)
    b_idx = jnp.arange(inner, dtype=jnp.int32)
    c_idx = jnp.arange(blocks, dtype=jnp.int32)
    w1 = angle(b_idx[:, None] * c_idx[None, :], inner)
    w1c, w1s = jnp.cos(w1), jnp.sin(w1)
    tw = angle(b_idx[:, None] * a_idx[None, :], lon_count)
    twc, tws = jnp.cos(tw)[:, :, None], jnp.sin(tw)[:, :, None]
    w2 = angle(a_idx[:, None] * a_idx[None, :], outer)
    w2c, w2s = jnp.cos(w2), jnp.sin(w2)

    def mm(spec, left, right):
        return jnp.einsum(spec, left, right, precision=highest)

    rot1 = jnp.stack([jnp.stack([w1c, -w1s]), jnp.stack([w1s, w1c])])
    y = mm("kjbc,jdcq->kbdq", rot1, x_parts)
    t_re = y[0] * twc - y[1] * tws
    t_im = y[0] * tws + y[1] * twc
    field = mm("jad,jbdq->abq", jnp.stack([w2c, -w2s]), jnp.stack([t_re, t_im]))
    squared = (field * field).astype(jnp.bfloat16)
    sq = squared.astype(jnp.float32)
    z = mm("kda,abq->kbdq", jnp.stack([w2c, -w2s]), sq)
    u_re = z[0] * twc + z[1] * tws
    u_im = z[1] * twc - z[0] * tws
    rot2 = jnp.stack([jnp.stack([w1c, w1s]), jnp.stack([-w1s, w1c])])
    f = mm("kjbc,jbdq->kcdq", rot2, jnp.stack([u_re, u_im]))
    first = (c_idx[:, None] == 0) & (a_idx[None, :] == 0)
    scaling = jnp.where(first, 1.0, 2.0).astype(jnp.float32)[:, :, None] / lon_count
    four_cos = f[0] * scaling
    four_sin = -f[1] * scaling
    grid = jnp.transpose(squared, (2, 0, 1)).reshape(signals, lon_count)
    return grid, four_cos, four_sin


def shards(coeffs, legendre, orders, lat_map, weights):
    slot_cap = coeffs.shape[0]
    epoch_count = coeffs.shape[1]
    deg_count = legendre.shape[1]
    half_lats = legendre.shape[2]
    lon_count = 2 * deg_count
    lat_rows = lat_map.shape[0]
    devices = lax.axis_size(("gx", "gy"))
    rows_each = lat_rows // devices

    synth = synthesize(coeffs, legendre, orders).reshape(slot_cap, 2, epoch_count * 2, half_lats)
    full_lats = jnp.concatenate([synth[:, 0], synth[:, 1, :, ::-1]], axis=-1)

    onehot = one_hot_rows(lat_map, lat_rows)
    permuted = jnp.einsum(
        "sxk,kr->sxr", full_lats, onehot, preferred_element_type=jnp.float32
    ).astype(jnp.bfloat16)
    sends = permuted.reshape(slot_cap, epoch_count * 2, devices, rows_each)
    sends = jnp.transpose(sends, (2, 0, 1, 3)).reshape(devices, slot_cap, epoch_count * 2 * rows_each)
    inner = inner_length(lon_count)
    outer = lon_count // inner
    blocks = deg_count // outer
    block_of = jnp.where(orders >= 0, orders // outer, -1)
    order_code = jnp.stack([block_of, orders % outer], axis=-1).astype(jnp.bfloat16)
    order_code = jnp.broadcast_to(order_code[None], (devices, slot_cap, 2))
    payload = jnp.concatenate([sends, order_code], axis=-1).reshape(devices, -1)
    width = payload.shape[1]
    padded = -(-width // 256) * 256
    payload = jnp.pad(payload, ((0, 0), (0, padded - width))).reshape(devices, padded // 128, 128)
    got = lax.all_to_all(payload, ("gx", "gy"), 0, 0, tiled=True)
    got = got.reshape(devices, padded)[:, :width].reshape(devices * slot_cap, -1)
    code = got[:, -2:].astype(jnp.int32)
    data = got[:, :-2]
    by_d = (code[:, 1:2] == jnp.arange(outer, dtype=jnp.int32)[None, :]).astype(jnp.bfloat16)
    in_c = code[:, 0:1] == jnp.arange(blocks, dtype=jnp.int32)[None, :]
    spread = jnp.where(in_c[:, :, None], data[:, None, :], jnp.zeros((), jnp.bfloat16))
    dense = jnp.einsum("sd,scr->dcr", by_d, spread, preferred_element_type=jnp.float32)
    dense = dense.reshape(outer, blocks, epoch_count, 2, rows_each)
    x_parts = jnp.stack([dense[:, :, :, 0, :], -dense[:, :, :, 1, :]])
    x_parts = x_parts.reshape(2, outer, blocks, epoch_count * rows_each)
    grid, four_cos, four_sin = transform_blocks(x_parts, lon_count)
    grid_rows = jnp.transpose(grid.reshape(epoch_count, rows_each, lon_count), (1, 0, 2))

    split = (blocks, outer, epoch_count, rows_each)
    fourier = jnp.stack([four_cos.reshape(split), four_sin.reshape(split)], axis=3)
    fourier = fourier.astype(jnp.bfloat16).reshape(blocks, outer, -1)
    picked = jnp.einsum("sd,cdr->scr", by_d, fourier, preferred_element_type=jnp.float32)
    by_slot = jnp.sum(jnp.where(in_c[:, :, None], picked, jnp.float32(0.0)), axis=1)
    back = by_slot.astype(jnp.bfloat16).reshape(devices, -1)
    width = back.shape[1]
    padded = -(-width // 256) * 256
    back = jnp.pad(back, ((0, 0), (0, padded - width))).reshape(devices, padded // 128, 128)
    back = lax.all_to_all(back, ("gx", "gy"), 0, 0, tiled=True)
    back = back.reshape(devices, padded)[:, :width].reshape(devices, slot_cap, epoch_count, 2, rows_each)
    returned = jnp.transpose(back, (1, 2, 3, 0, 4)).reshape(slot_cap, epoch_count * 2, lat_rows)
    natural = jnp.einsum(
        "sxr,kr->sxk", returned, onehot, preferred_element_type=jnp.float32
    )
    northern = natural[..., :half_lats]
    southern = natural[..., half_lats:][..., ::-1]
    sym_part = ((northern + southern) * weights).astype(jnp.bfloat16)
    anti_part = ((northern - southern) * weights).astype(jnp.bfloat16)
    both = jnp.concatenate([sym_part, anti_part], axis=1)
    spectra = analyze(both, legendre, orders, epoch_count, 2)
    return (grid_rows, spectra)


def solution(mesh):
    placed = (
        P(("gx", "gy"), None, None, None),
        P(("gx", "gy"), None, None),
        P(("gx", "gy")),
        P(),
        P(),
    )
    return jax.shard_map(
        shards,
        mesh=mesh,
        in_specs=placed,
        out_specs=(P(("gx", "gy"), None, None), P(("gx", "gy"), None, None, None)),
        check_vma=False,
    )
```

```python
import math

import jax
import jax.numpy as jnp
from jax import lax
from jax.experimental import pallas as pl
from jax.experimental.pallas import tpu as pltpu
from jax.sharding import PartitionSpec as P


SLOTS_PER_STEP = 6


def _masks(order, first, width):
    degrees = first + lax.broadcasted_iota(jnp.int32, (1, width), 1)
    usable = degrees >= order
    even = ((degrees + order) & 1) == 0
    return usable, even


def _chunks(deg_count):
    bounds = list(range(0, deg_count, 256)) + [deg_count]
    return list(zip(bounds[:-1], bounds[1:]))


def _synth_kernel(orders_ref, coef_ref, leg_ref, out_ref, acc_ref):
    step = pl.program_id(0)
    block, epochs, _, deg_count = coef_ref.shape
    zero = jnp.zeros((), coef_ref.dtype)
    for i in range(block):
        order = orders_ref[step * block + i]
        acc_ref[...] = jnp.zeros_like(acc_ref)
        for lo, hi in _chunks(deg_count):

            @pl.when((order >= 0) & (order < hi))
            def _(i=i, lo=lo, hi=hi, order=order):
                usable, even = _masks(order, lo, hi - lo)
                rows = jnp.concatenate([coef_ref[i, e, :, lo:hi] for e in range(epochs)], axis=0)
                masked = jnp.where(usable, rows, zero)
                signed = jnp.where(even, masked, -masked)
                lhs = jnp.concatenate([masked, signed], axis=0)
                acc_ref[...] += jnp.dot(lhs, leg_ref[i, lo:hi, :], preferred_element_type=jnp.float32)

        out_ref[i] = acc_ref[...].astype(out_ref.dtype)


def synthesize(coeffs, legendre, orders):
    slot_cap, epochs, parts, deg_count = coeffs.shape
    half_lats = legendre.shape[2]
    block = SLOTS_PER_STEP
    rows = 2 * epochs * parts
    grid_spec = pltpu.PrefetchScalarGridSpec(
        num_scalar_prefetch=1,
        grid=(slot_cap // block,),
        in_specs=[
            pl.BlockSpec((block, epochs, parts, deg_count), lambda g, o: (g, 0, 0, 0)),
            pl.BlockSpec((block, deg_count, half_lats), lambda g, o: (g, 0, 0)),
        ],
        out_specs=pl.BlockSpec((block, rows, half_lats), lambda g, o: (g, 0, 0)),
        scratch_shapes=[pltpu.VMEM((rows, half_lats), jnp.float32)],
    )
    return pl.pallas_call(
        _synth_kernel,
        grid_spec=grid_spec,
        out_shape=jax.ShapeDtypeStruct((slot_cap, rows, half_lats), jnp.bfloat16),
        compiler_params=pltpu.CompilerParams(dimension_semantics=("arbitrary",)),
        cost_estimate=pl.CostEstimate(
            flops=2 * slot_cap * rows * deg_count * half_lats,
            bytes_accessed=legendre.size * 2 + coeffs.size * 2 + slot_cap * rows * half_lats * 2,
            transcendentals=0,
        ),
    )(orders, coeffs, legendre)


def _analysis_kernel(orders_ref, both_ref, leg_ref, out_ref):
    step = pl.program_id(0)
    block, epochs, parts, deg_count = out_ref.shape
    half = epochs * parts
    for i in range(block):
        order = orders_ref[step * block + i]
        for lo, hi in _chunks(deg_count):
            needed = (order >= 0) & (order < hi)

            @pl.when(needed)
            def _(i=i, lo=lo, hi=hi, order=order):
                usable, even = _masks(order, lo, hi - lo)
                res = lax.dot_general(
                    both_ref[i], leg_ref[i, lo:hi, :], (((1,), (1,)), ((), ())),
                    preferred_element_type=jnp.float32,
                )
                chosen = jnp.where(even, res[:half], res[half:])
                chosen = jnp.where(usable, chosen, jnp.float32(0.0)).astype(out_ref.dtype)
                for e in range(epochs):
                    out_ref[i, e, :, lo:hi] = chosen[e * parts:(e + 1) * parts]

            @pl.when(jnp.logical_not(needed))
            def _(i=i, lo=lo, hi=hi):
                out_ref[i, :, :, lo:hi] = jnp.zeros((epochs, parts, hi - lo), out_ref.dtype)


def analyze(both, legendre, orders, epochs, parts):
    slot_cap, rows, half_lats = both.shape
    deg_count = legendre.shape[1]
    block = SLOTS_PER_STEP
    grid_spec = pltpu.PrefetchScalarGridSpec(
        num_scalar_prefetch=1,
        grid=(slot_cap // block,),
        in_specs=[
            pl.BlockSpec((block, rows, half_lats), lambda g, o: (g, 0, 0)),
            pl.BlockSpec((block, deg_count, half_lats), lambda g, o: (g, 0, 0)),
        ],
        out_specs=pl.BlockSpec((block, epochs, parts, deg_count), lambda g, o: (g, 0, 0, 0)),
    )
    return pl.pallas_call(
        _analysis_kernel,
        grid_spec=grid_spec,
        out_shape=jax.ShapeDtypeStruct((slot_cap, epochs, parts, deg_count), jnp.bfloat16),
        compiler_params=pltpu.CompilerParams(dimension_semantics=("arbitrary",)),
        cost_estimate=pl.CostEstimate(
            flops=2 * slot_cap * rows * deg_count * half_lats,
            bytes_accessed=legendre.size * 2 + both.size * 2 + slot_cap * epochs * parts * deg_count * 2,
            transcendentals=0,
        ),
    )(orders, both, legendre)


def inner_length(lon_count):
    best = 1
    for factor in range(1, math.isqrt(lon_count) + 1):
        if lon_count % factor == 0:
            best = factor
    return best


def one_hot_rows(lat_map, lat_rows):
    return (lat_map[None, :] == jnp.arange(lat_rows, dtype=jnp.int32)[:, None]).astype(jnp.bfloat16)


def angle(numer, denom):
    return jnp.float32(2.0 * math.pi) * (numer % denom).astype(jnp.float32) / jnp.float32(denom)


def transform_blocks(x_parts, lon_count):
    highest = lax.Precision.HIGHEST
    _, outer, blocks, signals = x_parts.shape
    inner = lon_count // outer
    a_idx = jnp.arange(outer, dtype=jnp.int32)
    b_idx = jnp.arange(inner, dtype=jnp.int32)
    c_idx = jnp.arange(blocks, dtype=jnp.int32)
    w1 = angle(b_idx[:, None] * c_idx[None, :], inner)
    w1c, w1s = jnp.cos(w1), jnp.sin(w1)
    tw = angle(b_idx[:, None] * a_idx[None, :], lon_count)
    twc, tws = jnp.cos(tw)[:, :, None], jnp.sin(tw)[:, :, None]
    w2 = angle(a_idx[:, None] * a_idx[None, :], outer)
    w2c, w2s = jnp.cos(w2), jnp.sin(w2)

    def mm(spec, left, right):
        return jnp.einsum(spec, left, right, precision=highest)

    rot1 = jnp.stack([jnp.stack([w1c, -w1s]), jnp.stack([w1s, w1c])])
    y = mm("kjbc,jdcq->kbdq", rot1, x_parts)
    t_re = y[0] * twc - y[1] * tws
    t_im = y[0] * tws + y[1] * twc
    field = mm("jad,jbdq->abq", jnp.stack([w2c, -w2s]), jnp.stack([t_re, t_im]))
    squared = (field * field).astype(jnp.bfloat16)
    sq = squared.astype(jnp.float32)
    z = mm("kda,abq->kbdq", jnp.stack([w2c, -w2s]), sq)
    u_re = z[0] * twc + z[1] * tws
    u_im = z[1] * twc - z[0] * tws
    rot2 = jnp.stack([jnp.stack([w1c, w1s]), jnp.stack([-w1s, w1c])])
    f = mm("kjbc,jbdq->kcdq", rot2, jnp.stack([u_re, u_im]))
    first = (c_idx[:, None] == 0) & (a_idx[None, :] == 0)
    scaling = jnp.where(first, 1.0, 2.0).astype(jnp.float32)[:, :, None] / lon_count
    four_cos = f[0] * scaling
    four_sin = -f[1] * scaling
    grid = jnp.transpose(squared, (2, 0, 1)).reshape(signals, lon_count)
    return grid, four_cos, four_sin


def shards(coeffs, legendre, orders, lat_map, weights):
    slot_cap = coeffs.shape[0]
    epoch_count = coeffs.shape[1]
    deg_count = legendre.shape[1]
    half_lats = legendre.shape[2]
    lon_count = 2 * deg_count
    lat_rows = lat_map.shape[0]
    devices = lax.axis_size(("gx", "gy"))
    rows_each = lat_rows // devices

    synth = synthesize(coeffs, legendre, orders).reshape(slot_cap, 2, epoch_count * 2, half_lats)
    full_lats = jnp.concatenate([synth[:, 0], synth[:, 1, :, ::-1]], axis=-1)

    onehot = one_hot_rows(lat_map, lat_rows)
    permuted = jnp.einsum(
        "sxk,kr->sxr", full_lats, onehot, preferred_element_type=jnp.float32
    ).astype(jnp.bfloat16)
    sends = permuted.reshape(slot_cap, epoch_count * 2, devices, rows_each)
    sends = jnp.transpose(sends, (2, 0, 1, 3)).reshape(devices, slot_cap, epoch_count * 2 * rows_each)
    inner = inner_length(lon_count)
    outer = lon_count // inner
    blocks = deg_count // outer
    block_of = jnp.where(orders >= 0, orders // outer, -1)
    order_code = jnp.stack([block_of, orders % outer], axis=-1).astype(jnp.bfloat16)
    order_code = jnp.broadcast_to(order_code[None], (devices, slot_cap, 2))
    payload = jnp.concatenate([sends, order_code], axis=-1).reshape(devices, -1)
    width = payload.shape[1]
    padded = -(-width // 256) * 256
    payload = jnp.pad(payload, ((0, 0), (0, padded - width))).reshape(devices, padded // 128, 128)
    got = lax.all_to_all(payload, ("gx", "gy"), 0, 0, tiled=True)
    got = got.reshape(devices, padded)[:, :width].reshape(devices * slot_cap, -1)
    code = got[:, -2:].astype(jnp.int32)
    data = got[:, :-2]
    by_d = (code[:, 1:2] == jnp.arange(outer, dtype=jnp.int32)[None, :]).astype(jnp.bfloat16)
    in_c = code[:, 0:1] == jnp.arange(blocks, dtype=jnp.int32)[None, :]
    spread = jnp.where(in_c[:, :, None], data[:, None, :], jnp.zeros((), jnp.bfloat16))
    dense = jnp.einsum("sd,scr->dcr", by_d, spread, preferred_element_type=jnp.float32)
    dense = dense.reshape(outer, blocks, epoch_count, 2, rows_each)
    x_parts = jnp.stack([dense[:, :, :, 0, :], -dense[:, :, :, 1, :]])
    x_parts = x_parts.reshape(2, outer, blocks, epoch_count * rows_each)
    grid, four_cos, four_sin = transform_blocks(x_parts, lon_count)
    grid_rows = jnp.transpose(grid.reshape(epoch_count, rows_each, lon_count), (1, 0, 2))

    split = (blocks, outer, epoch_count, rows_each)
    fourier = jnp.stack([four_cos.reshape(split), four_sin.reshape(split)], axis=3)
    fourier = fourier.astype(jnp.bfloat16).reshape(blocks, outer, -1)
    picked = jnp.einsum("sd,cdr->scr", by_d, fourier, preferred_element_type=jnp.float32)
    by_slot = jnp.sum(jnp.where(in_c[:, :, None], picked, jnp.float32(0.0)), axis=1)
    back = by_slot.astype(jnp.bfloat16).reshape(devices, -1)
    width = back.shape[1]
    padded = -(-width // 256) * 256
    back = jnp.pad(back, ((0, 0), (0, padded - width))).reshape(devices, padded // 128, 128)
    back = lax.all_to_all(back, ("gx", "gy"), 0, 0, tiled=True)
    back = back.reshape(devices, padded)[:, :width].reshape(devices, slot_cap, epoch_count, 2, rows_each)
    returned = jnp.transpose(back, (1, 2, 3, 0, 4)).reshape(slot_cap, epoch_count * 2, lat_rows)
    natural = jnp.einsum(
        "sxr,kr->sxk", returned, onehot, preferred_element_type=jnp.float32
    )
    northern = natural[..., :half_lats]
    southern = natural[..., half_lats:][..., ::-1]
    sym_part = ((northern + southern) * weights).astype(jnp.bfloat16)
    anti_part = ((northern - southern) * weights).astype(jnp.bfloat16)
    both = jnp.concatenate([sym_part, anti_part], axis=1)
    spectra = analyze(both, legendre, orders, epoch_count, 2)
    return (grid_rows, spectra)


def solution(mesh):
    placed = (
        P(("gx", "gy"), None, None, None),
        P(("gx", "gy"), None, None),
        P(("gx", "gy")),
        P(),
        P(),
    )
    return jax.shard_map(
        shards,
        mesh=mesh,
        in_specs=placed,
        out_specs=(P(("gx", "gy"), None, None), P(("gx", "gy"), None, None, None)),
        check_vma=False,
    )
```

```python
import math

import jax
import jax.numpy as jnp
from jax import lax
from jax.experimental import pallas as pl
from jax.experimental.pallas import tpu as pltpu
from jax.sharding import PartitionSpec as P


SLOTS_PER_STEP = 12


def _masks(order, deg_count):
    degrees = lax.broadcasted_iota(jnp.int32, (1, deg_count), 1)
    usable = (degrees >= order) & (order >= 0)
    even = ((degrees + order) & 1) == 0
    return usable, even


def _synth_kernel(orders_ref, coef_ref, leg_ref, out_ref):
    step = pl.program_id(0)
    block, epochs, _, deg_count = coef_ref.shape
    zero = jnp.zeros((), coef_ref.dtype)
    for i in range(block):
        order = orders_ref[step * block + i]
        usable, even = _masks(order, deg_count)
        rows = jnp.concatenate([coef_ref[i, e] for e in range(epochs)], axis=0)
        masked = jnp.where(usable, rows, zero)
        signed = jnp.where(even, masked, -masked)
        lhs = jnp.concatenate([masked, signed], axis=0)
        out_ref[i] = jnp.dot(lhs, leg_ref[i], preferred_element_type=jnp.float32).astype(out_ref.dtype)


def synthesize(coeffs, legendre, orders):
    slot_cap, epochs, parts, deg_count = coeffs.shape
    half_lats = legendre.shape[2]
    block = SLOTS_PER_STEP
    rows = 2 * epochs * parts
    grid_spec = pltpu.PrefetchScalarGridSpec(
        num_scalar_prefetch=1,
        grid=(slot_cap // block,),
        in_specs=[
            pl.BlockSpec((block, epochs, parts, deg_count), lambda g, o: (g, 0, 0, 0)),
            pl.BlockSpec((block, deg_count, half_lats), lambda g, o: (g, 0, 0)),
        ],
        out_specs=pl.BlockSpec((block, rows, half_lats), lambda g, o: (g, 0, 0)),
    )
    return pl.pallas_call(
        _synth_kernel,
        grid_spec=grid_spec,
        out_shape=jax.ShapeDtypeStruct((slot_cap, rows, half_lats), jnp.bfloat16),
        compiler_params=pltpu.CompilerParams(dimension_semantics=("arbitrary",)),
        cost_estimate=pl.CostEstimate(
            flops=2 * slot_cap * rows * deg_count * half_lats,
            bytes_accessed=legendre.size * 2 + coeffs.size * 2 + slot_cap * rows * half_lats * 2,
            transcendentals=0,
        ),
    )(orders, coeffs, legendre)


def _analysis_kernel(orders_ref, both_ref, leg_ref, out_ref):
    step = pl.program_id(0)
    block, epochs, parts, deg_count = out_ref.shape
    half = epochs * parts
    for i in range(block):
        order = orders_ref[step * block + i]
        usable, even = _masks(order, deg_count)
        res = lax.dot_general(
            both_ref[i], leg_ref[i], (((1,), (1,)), ((), ())), preferred_element_type=jnp.float32
        )
        chosen = jnp.where(even, res[:half], res[half:])
        chosen = jnp.where(usable, chosen, jnp.float32(0.0)).astype(out_ref.dtype)
        for e in range(epochs):
            out_ref[i, e] = chosen[e * parts:(e + 1) * parts]


def analyze(both, legendre, orders, epochs, parts):
    slot_cap, rows, half_lats = both.shape
    deg_count = legendre.shape[1]
    block = SLOTS_PER_STEP
    grid_spec = pltpu.PrefetchScalarGridSpec(
        num_scalar_prefetch=1,
        grid=(slot_cap // block,),
        in_specs=[
            pl.BlockSpec((block, rows, half_lats), lambda g, o: (g, 0, 0)),
            pl.BlockSpec((block, deg_count, half_lats), lambda g, o: (g, 0, 0)),
        ],
        out_specs=pl.BlockSpec((block, epochs, parts, deg_count), lambda g, o: (g, 0, 0, 0)),
    )
    return pl.pallas_call(
        _analysis_kernel,
        grid_spec=grid_spec,
        out_shape=jax.ShapeDtypeStruct((slot_cap, epochs, parts, deg_count), jnp.bfloat16),
        compiler_params=pltpu.CompilerParams(dimension_semantics=("arbitrary",)),
        cost_estimate=pl.CostEstimate(
            flops=2 * slot_cap * rows * deg_count * half_lats,
            bytes_accessed=legendre.size * 2 + both.size * 2 + slot_cap * epochs * parts * deg_count * 2,
            transcendentals=0,
        ),
    )(orders, both, legendre)


def inner_length(lon_count):
    best = 1
    for factor in range(1, math.isqrt(lon_count) + 1):
        if lon_count % factor == 0:
            best = factor
    return best


def one_hot_rows(lat_map, lat_rows):
    return (lat_map[None, :] == jnp.arange(lat_rows, dtype=jnp.int32)[:, None]).astype(jnp.bfloat16)


def angle(numer, denom):
    return jnp.float32(2.0 * math.pi) * (numer % denom).astype(jnp.float32) / jnp.float32(denom)


def transform_blocks(x_parts, lon_count):
    highest = lax.Precision.HIGHEST
    _, outer, blocks, signals = x_parts.shape
    inner = lon_count // outer
    a_idx = jnp.arange(outer, dtype=jnp.int32)
    b_idx = jnp.arange(inner, dtype=jnp.int32)
    c_idx = jnp.arange(blocks, dtype=jnp.int32)
    w1 = angle(b_idx[:, None] * c_idx[None, :], inner)
    w1c, w1s = jnp.cos(w1), jnp.sin(w1)
    tw = angle(b_idx[:, None] * a_idx[None, :], lon_count)
    twc, tws = jnp.cos(tw)[:, :, None], jnp.sin(tw)[:, :, None]
    w2 = angle(a_idx[:, None] * a_idx[None, :], outer)
    w2c, w2s = jnp.cos(w2), jnp.sin(w2)

    def mm(spec, left, right):
        return jnp.einsum(spec, left, right, precision=highest)

    rot1 = jnp.stack([jnp.stack([w1c, -w1s]), jnp.stack([w1s, w1c])])
    y = mm("kjbc,jdcq->kbdq", rot1, x_parts)
    t_re = y[0] * twc - y[1] * tws
    t_im = y[0] * tws + y[1] * twc
    field = mm("jad,jbdq->abq", jnp.stack([w2c, -w2s]), jnp.stack([t_re, t_im]))
    squared = (field * field).astype(jnp.bfloat16)
    sq = squared.astype(jnp.float32)
    z = mm("kda,abq->kbdq", jnp.stack([w2c, -w2s]), sq)
    u_re = z[0] * twc + z[1] * tws
    u_im = z[1] * twc - z[0] * tws
    rot2 = jnp.stack([jnp.stack([w1c, w1s]), jnp.stack([-w1s, w1c])])
    f = mm("kjbc,jbdq->kcdq", rot2, jnp.stack([u_re, u_im]))
    first = (c_idx[:, None] == 0) & (a_idx[None, :] == 0)
    scaling = jnp.where(first, 1.0, 2.0).astype(jnp.float32)[:, :, None] / lon_count
    four_cos = f[0] * scaling
    four_sin = -f[1] * scaling
    grid = jnp.transpose(squared, (2, 0, 1)).reshape(signals, lon_count)
    return grid, four_cos, four_sin


def shards(coeffs, legendre, orders, lat_map, weights):
    slot_cap = coeffs.shape[0]
    epoch_count = coeffs.shape[1]
    deg_count = legendre.shape[1]
    half_lats = legendre.shape[2]
    lon_count = 2 * deg_count
    lat_rows = lat_map.shape[0]
    devices = lax.axis_size(("gx", "gy"))
    rows_each = lat_rows // devices

    synth = synthesize(coeffs, legendre, orders).reshape(slot_cap, 2, epoch_count * 2, half_lats)
    full_lats = jnp.concatenate([synth[:, 0], synth[:, 1, :, ::-1]], axis=-1)

    onehot = one_hot_rows(lat_map, lat_rows)
    permuted = jnp.einsum(
        "sxk,kr->sxr", full_lats, onehot, preferred_element_type=jnp.float32
    ).astype(jnp.bfloat16)
    sends = permuted.reshape(slot_cap, epoch_count * 2, devices, rows_each)
    sends = jnp.transpose(sends, (2, 0, 1, 3)).reshape(devices, slot_cap, epoch_count * 2 * rows_each)
    inner = inner_length(lon_count)
    outer = lon_count // inner
    blocks = deg_count // outer
    block_of = jnp.where(orders >= 0, orders // outer, -1)
    order_code = jnp.stack([block_of, orders % outer], axis=-1).astype(jnp.bfloat16)
    order_code = jnp.broadcast_to(order_code[None], (devices, slot_cap, 2))
    payload = jnp.concatenate([sends, order_code], axis=-1).reshape(devices, -1)
    width = payload.shape[1]
    padded = -(-width // 256) * 256
    payload = jnp.pad(payload, ((0, 0), (0, padded - width))).reshape(devices, padded // 128, 128)
    got = lax.all_to_all(payload, ("gx", "gy"), 0, 0, tiled=True)
    got = got.reshape(devices, padded)[:, :width].reshape(devices * slot_cap, -1)
    data = got[:, :-2]
    by_d = (got[:, -1:] == jnp.arange(outer, dtype=jnp.bfloat16)[None, :]).astype(jnp.bfloat16)
    in_c = got[:, -2:-1] == jnp.arange(blocks, dtype=jnp.bfloat16)[None, :]
    spread = jnp.where(in_c[:, :, None], data[:, None, :], jnp.zeros((), jnp.bfloat16))
    dense = jnp.einsum("sd,scr->dcr", by_d, spread, preferred_element_type=jnp.float32)
    dense = dense.reshape(outer, blocks, epoch_count, 2, rows_each)
    x_parts = jnp.stack([dense[:, :, :, 0, :], -dense[:, :, :, 1, :]])
    x_parts = jnp.transpose(x_parts, (0, 1, 2, 4, 3)).reshape(2, outer, blocks, rows_each * epoch_count)
    grid, four_cos, four_sin = transform_blocks(x_parts, lon_count)
    grid_rows = grid.reshape(rows_each, epoch_count, lon_count)

    split = (blocks, outer, rows_each, epoch_count)
    fourier = jnp.stack([four_cos.reshape(split), four_sin.reshape(split)], axis=4)
    fourier = jnp.transpose(fourier, (0, 1, 3, 4, 2))
    fourier = fourier.astype(jnp.bfloat16).reshape(blocks, outer, -1)
    picked = jnp.einsum("sd,cdr->scr", by_d, fourier, preferred_element_type=jnp.float32)
    by_slot = jnp.sum(jnp.where(in_c[:, :, None], picked, jnp.float32(0.0)), axis=1)
    back = by_slot.astype(jnp.bfloat16).reshape(devices, -1)
    width = back.shape[1]
    padded = -(-width // 256) * 256
    back = jnp.pad(back, ((0, 0), (0, padded - width))).reshape(devices, padded // 128, 128)
    back = lax.all_to_all(back, ("gx", "gy"), 0, 0, tiled=True)
    back = back.reshape(devices, padded)[:, :width].reshape(devices, slot_cap, epoch_count, 2, rows_each)
    returned = jnp.transpose(back, (1, 2, 3, 0, 4)).reshape(slot_cap, epoch_count * 2, lat_rows)
    natural = jnp.einsum(
        "sxr,kr->sxk", returned, onehot, preferred_element_type=jnp.float32
    )
    northern = natural[..., :half_lats]
    southern = natural[..., half_lats:][..., ::-1]
    sym_part = ((northern + southern) * weights).astype(jnp.bfloat16)
    anti_part = ((northern - southern) * weights).astype(jnp.bfloat16)
    both = jnp.concatenate([sym_part, anti_part], axis=1)
    spectra = analyze(both, legendre, orders, epoch_count, 2)
    return (grid_rows, spectra)


def solution(mesh):
    placed = (
        P(("gx", "gy"), None, None, None),
        P(("gx", "gy"), None, None),
        P(("gx", "gy")),
        P(),
        P(),
    )
    return jax.shard_map(
        shards,
        mesh=mesh,
        in_specs=placed,
        out_specs=(P(("gx", "gy"), None, None), P(("gx", "gy"), None, None, None)),
        check_vma=False,
    )
```

```python
import math

import jax
import jax.numpy as jnp
from jax import lax
from jax.experimental import pallas as pl
from jax.experimental.pallas import tpu as pltpu
from jax.sharding import PartitionSpec as P


SLOTS_PER_STEP = 12


def _masks(order, deg_count):
    degrees = lax.broadcasted_iota(jnp.int32, (1, deg_count), 1)
    usable = (degrees >= order) & (order >= 0)
    even = ((degrees + order) & 1) == 0
    return usable, even


def _synth_kernel(orders_ref, coef_ref, leg_ref, out_ref):
    step = pl.program_id(0)
    block, epochs, _, deg_count = coef_ref.shape
    zero = jnp.zeros((), coef_ref.dtype)
    for i in range(block):
        order = orders_ref[step * block + i]
        usable, even = _masks(order, deg_count)
        rows = jnp.concatenate([coef_ref[i, e] for e in range(epochs)], axis=0)
        masked = jnp.where(usable, rows, zero)
        signed = jnp.where(even, masked, -masked)
        lhs = jnp.concatenate([masked, signed], axis=0)
        out_ref[i] = jnp.dot(lhs, leg_ref[i], preferred_element_type=jnp.float32).astype(out_ref.dtype)


def _payload_kernel(orders_ref, coef_ref, leg_ref, aux_ref, out_ref, north_ref, south_ref):
    step = pl.program_id(0)
    block, epochs, _, deg_count = coef_ref.shape
    steps = orders_ref.shape[0] // block
    per = 2 * epochs
    half_lats = leg_ref.shape[2]
    devices, width = out_ref.shape
    rows_each = width // 128 - 2
    zero = jnp.zeros((), coef_ref.dtype)

    @pl.when(step == 0)
    def _():
        north_ref[...] = jnp.zeros_like(north_ref)
        south_ref[...] = jnp.zeros_like(south_ref)

    for i in range(block):
        order = orders_ref[step * block + i]
        usable, even = _masks(order, deg_count)
        rows = jnp.concatenate([coef_ref[i, e] for e in range(epochs)], axis=0)
        masked = jnp.where(usable, rows, zero)
        signed = jnp.where(even, masked, -masked)
        lhs = jnp.concatenate([masked, signed], axis=0)
        res = jnp.dot(lhs, leg_ref[i], preferred_element_type=jnp.float32)
        res = res.astype(jnp.bfloat16).astype(jnp.float32)
        for g in range(steps):

            @pl.when(step == g)
            def _(g=g, i=i, res=res):
                first = (g * block + i) * per
                north_ref[first:first + per, :] = res[:per]
                south_ref[first:first + per, :] = res[per:]

    @pl.when(step == steps - 1)
    def _():
        lat = lax.broadcasted_iota(jnp.int32, (half_lats, 1), 0)
        north = north_ref[...].astype(jnp.bfloat16)
        south = south_ref[...].astype(jnp.bfloat16)
        dims = (((1,), (1,)), ((), ()))
        for t in range(rows_each):
            held = aux_ref[t:t + 1, :]
            pick_n = (held == lat).astype(jnp.float32).T.astype(jnp.bfloat16)
            pick_s = (held == 2 * half_lats - 1 - lat).astype(jnp.float32).T.astype(jnp.bfloat16)
            rows_t = lax.dot_general(pick_n, north, dims, preferred_element_type=jnp.float32)
            rows_t += lax.dot_general(pick_s, south, dims, preferred_element_type=jnp.float32)
            out_ref[:, t * 128:(t + 1) * 128] = rows_t.astype(out_ref.dtype)
        for j in range(2):
            code = aux_ref[rows_each + j:rows_each + j + 1, :].astype(jnp.float32)
            out_ref[:, (rows_each + j) * 128:(rows_each + j + 1) * 128] = jnp.broadcast_to(
                code, (devices, 128)
            ).astype(out_ref.dtype)


def synthesize_payload(coeffs, legendre, orders, aux, devices):
    slot_cap, epochs, parts, deg_count = coeffs.shape
    half_lats = legendre.shape[2]
    block = SLOTS_PER_STEP
    rows_each = aux.shape[0] - 2
    width = (rows_each + 2) * 128
    grid_spec = pltpu.PrefetchScalarGridSpec(
        num_scalar_prefetch=1,
        grid=(slot_cap // block,),
        in_specs=[
            pl.BlockSpec((block, epochs, parts, deg_count), lambda g, o: (g, 0, 0, 0)),
            pl.BlockSpec((block, deg_count, half_lats), lambda g, o: (g, 0, 0)),
            pl.BlockSpec(aux.shape, lambda g, o: (0, 0)),
        ],
        out_specs=pl.BlockSpec((devices, width), lambda g, o: (0, 0)),
        scratch_shapes=[pltpu.VMEM((128, half_lats), jnp.float32)] * 2,
    )
    rows = 2 * epochs * parts
    return pl.pallas_call(
        _payload_kernel,
        grid_spec=grid_spec,
        out_shape=jax.ShapeDtypeStruct((devices, width), jnp.bfloat16),
        compiler_params=pltpu.CompilerParams(dimension_semantics=("arbitrary",)),
        cost_estimate=pl.CostEstimate(
            flops=2 * slot_cap * rows * deg_count * half_lats,
            bytes_accessed=legendre.size * 2 + coeffs.size * 2 + devices * width * 2,
            transcendentals=0,
        ),
    )(orders, coeffs, legendre, aux)


def _analysis_kernel(orders_ref, both_ref, leg_ref, out_ref):
    step = pl.program_id(0)
    block, epochs, parts, deg_count = out_ref.shape
    half = epochs * parts
    for i in range(block):
        order = orders_ref[step * block + i]
        usable, even = _masks(order, deg_count)
        res = lax.dot_general(
            both_ref[i], leg_ref[i], (((1,), (1,)), ((), ())), preferred_element_type=jnp.float32
        )
        chosen = jnp.where(even, res[:half], res[half:])
        chosen = jnp.where(usable, chosen, jnp.float32(0.0)).astype(out_ref.dtype)
        for e in range(epochs):
            out_ref[i, e] = chosen[e * parts:(e + 1) * parts]


def analyze(both, legendre, orders, epochs, parts):
    slot_cap, rows, half_lats = both.shape
    deg_count = legendre.shape[1]
    block = SLOTS_PER_STEP
    grid_spec = pltpu.PrefetchScalarGridSpec(
        num_scalar_prefetch=1,
        grid=(slot_cap // block,),
        in_specs=[
            pl.BlockSpec((block, rows, half_lats), lambda g, o: (g, 0, 0)),
            pl.BlockSpec((block, deg_count, half_lats), lambda g, o: (g, 0, 0)),
        ],
        out_specs=pl.BlockSpec((block, epochs, parts, deg_count), lambda g, o: (g, 0, 0, 0)),
    )
    return pl.pallas_call(
        _analysis_kernel,
        grid_spec=grid_spec,
        out_shape=jax.ShapeDtypeStruct((slot_cap, epochs, parts, deg_count), jnp.bfloat16),
        compiler_params=pltpu.CompilerParams(dimension_semantics=("arbitrary",)),
        cost_estimate=pl.CostEstimate(
            flops=2 * slot_cap * rows * deg_count * half_lats,
            bytes_accessed=legendre.size * 2 + both.size * 2 + slot_cap * epochs * parts * deg_count * 2,
            transcendentals=0,
        ),
    )(orders, both, legendre)


def inner_length(lon_count):
    best = 1
    for factor in range(1, math.isqrt(lon_count) + 1):
        if lon_count % factor == 0:
            best = factor
    return best


def one_hot_rows(lat_map, lat_rows):
    return (lat_map[None, :] == jnp.arange(lat_rows, dtype=jnp.int32)[:, None]).astype(jnp.bfloat16)


def angle(numer, denom):
    return jnp.float32(2.0 * math.pi) * (numer % denom).astype(jnp.float32) / jnp.float32(denom)


def transform_blocks(x_parts, lon_count):
    highest = lax.Precision.HIGHEST
    _, outer, blocks, signals = x_parts.shape
    inner = lon_count // outer
    a_idx = jnp.arange(outer, dtype=jnp.int32)
    b_idx = jnp.arange(inner, dtype=jnp.int32)
    c_idx = jnp.arange(blocks, dtype=jnp.int32)
    w1 = angle(b_idx[:, None] * c_idx[None, :], inner)
    w1c, w1s = jnp.cos(w1), jnp.sin(w1)
    tw = angle(b_idx[:, None] * a_idx[None, :], lon_count)
    twc, tws = jnp.cos(tw)[:, :, None], jnp.sin(tw)[:, :, None]
    w2 = angle(a_idx[:, None] * a_idx[None, :], outer)
    w2c, w2s = jnp.cos(w2), jnp.sin(w2)

    def mm(spec, left, right):
        return jnp.einsum(spec, left, right, precision=highest)

    rot1 = jnp.stack([jnp.stack([w1c, -w1s]), jnp.stack([w1s, w1c])])
    y = mm("kjbc,jdcq->kbdq", rot1, x_parts)
    t_re = y[0] * twc - y[1] * tws
    t_im = y[0] * tws + y[1] * twc
    field = mm("jad,jbdq->abq", jnp.stack([w2c, -w2s]), jnp.stack([t_re, t_im]))
    squared = (field * field).astype(jnp.bfloat16)
    sq = squared.astype(jnp.float32)
    z = mm("kda,abq->kbdq", jnp.stack([w2c, -w2s]), sq)
    u_re = z[0] * twc + z[1] * tws
    u_im = z[1] * twc - z[0] * tws
    rot2 = jnp.stack([jnp.stack([w1c, w1s]), jnp.stack([-w1s, w1c])])
    f = mm("kjbc,jbdq->kcdq", rot2, jnp.stack([u_re, u_im]))
    first = (c_idx[:, None] == 0) & (a_idx[None, :] == 0)
    scaling = jnp.where(first, 1.0, 2.0).astype(jnp.float32)[:, :, None] / lon_count
    four_cos = f[0] * scaling
    four_sin = -f[1] * scaling
    grid = jnp.transpose(squared, (2, 0, 1)).reshape(signals, lon_count)
    return grid, four_cos, four_sin


def shards(coeffs, legendre, orders, lat_map, weights):
    slot_cap = coeffs.shape[0]
    epoch_count = coeffs.shape[1]
    deg_count = legendre.shape[1]
    half_lats = legendre.shape[2]
    lon_count = 2 * deg_count
    lat_rows = lat_map.shape[0]
    devices = lax.axis_size(("gx", "gy"))
    rows_each = lat_rows // devices

    inner = inner_length(lon_count)
    outer = lon_count // inner
    blocks = deg_count // outer
    assert slot_cap * 2 * epoch_count <= 128 and devices <= 128

    onehot = one_hot_rows(lat_map, lat_rows)

    lane_pad = 128 - slot_cap
    block_of = jnp.pad(jnp.where(orders >= 0, orders // outer, -1), (0, lane_pad), constant_values=-1)
    offset = jnp.pad(orders % outer, (0, lane_pad))
    lat_pairs = jnp.pad(jnp.transpose(lat_map.reshape(devices, rows_each)), ((0, 0), (0, 128 - devices)))
    aux = jnp.concatenate([lat_pairs, block_of[None], offset[None]], axis=0)
    payload = synthesize_payload(coeffs, legendre, orders, aux, devices)
    got = lax.all_to_all(payload, ("gx", "gy"), 0, 0, tiled=True)
    used = slot_cap * 2 * epoch_count
    data = jnp.stack([got[:, t * 128:t * 128 + used] for t in range(rows_each)], axis=1)
    data = jnp.transpose(data.reshape(devices, rows_each, slot_cap, -1), (0, 2, 1, 3))
    data = data.reshape(devices * slot_cap, -1)
    c_code = got[:, rows_each * 128:rows_each * 128 + slot_cap].reshape(-1, 1)
    d_code = got[:, (rows_each + 1) * 128:(rows_each + 1) * 128 + slot_cap].reshape(-1, 1)
    by_d = (d_code == jnp.arange(outer, dtype=jnp.bfloat16)[None, :]).astype(jnp.bfloat16)
    in_c = c_code == jnp.arange(blocks, dtype=jnp.bfloat16)[None, :]
    spread = jnp.where(in_c[:, :, None], data[:, None, :], jnp.zeros((), jnp.bfloat16))
    dense = jnp.einsum("sd,scr->dcr", by_d, spread, preferred_element_type=jnp.float32)
    dense = dense.reshape(outer, blocks, rows_each * epoch_count, 2)
    x_parts = jnp.stack([dense[..., 0], -dense[..., 1]])
    grid, four_cos, four_sin = transform_blocks(x_parts, lon_count)
    grid_rows = grid.reshape(rows_each, epoch_count, lon_count)

    split = (blocks, outer, rows_each, epoch_count)
    fourier = jnp.stack([four_cos.reshape(split), four_sin.reshape(split)], axis=4)
    fourier = jnp.transpose(fourier, (0, 1, 3, 4, 2))
    fourier = fourier.astype(jnp.bfloat16).reshape(blocks, outer, -1)
    picked = jnp.einsum("sd,cdr->scr", by_d, fourier, preferred_element_type=jnp.float32)
    by_slot = jnp.sum(jnp.where(in_c[:, :, None], picked, jnp.float32(0.0)), axis=1)
    back = by_slot.astype(jnp.bfloat16).reshape(devices, -1)
    width = back.shape[1]
    padded = -(-width // 256) * 256
    back = jnp.pad(back, ((0, 0), (0, padded - width))).reshape(devices, padded // 128, 128)
    back = lax.all_to_all(back, ("gx", "gy"), 0, 0, tiled=True)
    back = back.reshape(devices, padded)[:, :width].reshape(devices, slot_cap, epoch_count, 2, rows_each)
    returned = jnp.transpose(back, (1, 2, 3, 0, 4)).reshape(slot_cap, epoch_count * 2, lat_rows)
    natural = jnp.einsum(
        "sxr,kr->sxk", returned, onehot, preferred_element_type=jnp.float32
    )
    northern = natural[..., :half_lats]
    southern = natural[..., half_lats:][..., ::-1]
    sym_part = ((northern + southern) * weights).astype(jnp.bfloat16)
    anti_part = ((northern - southern) * weights).astype(jnp.bfloat16)
    both = jnp.concatenate([sym_part, anti_part], axis=1)
    spectra = analyze(both, legendre, orders, epoch_count, 2)
    return (grid_rows, spectra)


def solution(mesh):
    placed = (
        P(("gx", "gy"), None, None, None),
        P(("gx", "gy"), None, None),
        P(("gx", "gy")),
        P(),
        P(),
    )
    return jax.shard_map(
        shards,
        mesh=mesh,
        in_specs=placed,
        out_specs=(P(("gx", "gy"), None, None), P(("gx", "gy"), None, None, None)),
        check_vma=False,
    )
```

```python
import math

import jax
import jax.numpy as jnp
from jax import lax
from jax.experimental import pallas as pl
from jax.experimental.pallas import tpu as pltpu
from jax.sharding import PartitionSpec as P


SLOTS_PER_STEP = 12


def _masks(order, deg_count):
    degrees = lax.broadcasted_iota(jnp.int32, (1, deg_count), 1)
    usable = (degrees >= order) & (order >= 0)
    even = ((degrees + order) & 1) == 0
    return usable, even


def _synth_kernel(orders_ref, coef_ref, leg_ref, out_ref):
    step = pl.program_id(0)
    block, epochs, _, deg_count = coef_ref.shape
    zero = jnp.zeros((), coef_ref.dtype)
    for i in range(block):
        order = orders_ref[step * block + i]
        usable, even = _masks(order, deg_count)
        rows = jnp.concatenate([coef_ref[i, e] for e in range(epochs)], axis=0)
        masked = jnp.where(usable, rows, zero)
        signed = jnp.where(even, masked, -masked)
        lhs = jnp.concatenate([masked, signed], axis=0)
        out_ref[i] = jnp.dot(lhs, leg_ref[i], preferred_element_type=jnp.float32).astype(out_ref.dtype)


def synthesize(coeffs, legendre, orders):
    slot_cap, epochs, parts, deg_count = coeffs.shape
    half_lats = legendre.shape[2]
    block = SLOTS_PER_STEP
    rows = 2 * epochs * parts
    grid_spec = pltpu.PrefetchScalarGridSpec(
        num_scalar_prefetch=1,
        grid=(slot_cap // block,),
        in_specs=[
            pl.BlockSpec((block, epochs, parts, deg_count), lambda g, o: (g, 0, 0, 0)),
            pl.BlockSpec((block, deg_count, half_lats), lambda g, o: (g, 0, 0)),
        ],
        out_specs=pl.BlockSpec((block, rows, half_lats), lambda g, o: (g, 0, 0)),
    )
    return pl.pallas_call(
        _synth_kernel,
        grid_spec=grid_spec,
        out_shape=jax.ShapeDtypeStruct((slot_cap, rows, half_lats), jnp.bfloat16),
        compiler_params=pltpu.CompilerParams(dimension_semantics=("arbitrary",)),
        cost_estimate=pl.CostEstimate(
            flops=2 * slot_cap * rows * deg_count * half_lats,
            bytes_accessed=legendre.size * 2 + coeffs.size * 2 + slot_cap * rows * half_lats * 2,
            transcendentals=0,
        ),
    )(orders, coeffs, legendre)


def _analysis_kernel(orders_ref, ret_ref, pick_ref, w_ref, leg_ref, out_ref):
    step = pl.program_id(0)
    block, epochs, parts, deg_count = out_ref.shape
    half = epochs * parts
    held = ret_ref[...]
    north = jnp.dot(held, pick_ref[0], preferred_element_type=jnp.float32)
    south = jnp.dot(held, pick_ref[1], preferred_element_type=jnp.float32)
    sym = ((north + south) * w_ref[...]).astype(jnp.bfloat16).astype(jnp.float32)
    anti = ((north - south) * w_ref[...]).astype(jnp.bfloat16).astype(jnp.float32)
    for i in range(block):
        order = orders_ref[step * block + i]
        usable, even = _masks(order, deg_count)
        rows = slice(i * half, (i + 1) * half)
        both = jnp.concatenate([sym[rows], anti[rows]], axis=0).astype(jnp.bfloat16)
        res = lax.dot_general(
            both, leg_ref[i], (((1,), (1,)), ((), ())), preferred_element_type=jnp.float32
        )
        chosen = jnp.where(even, res[:half], res[half:])
        chosen = jnp.where(usable, chosen, jnp.float32(0.0)).astype(out_ref.dtype)
        for e in range(epochs):
            out_ref[i, e] = chosen[e * parts:(e + 1) * parts]


def analyze(returned, pick, weights, legendre, orders, epochs, parts):
    slot_cap = orders.shape[0]
    _, lat_rows = returned.shape
    deg_count, half_lats = legendre.shape[1:]
    block = SLOTS_PER_STEP
    half = epochs * parts
    grid_spec = pltpu.PrefetchScalarGridSpec(
        num_scalar_prefetch=1,
        grid=(slot_cap // block,),
        in_specs=[
            pl.BlockSpec((block * half, lat_rows), lambda g, o: (g, 0)),
            pl.BlockSpec(pick.shape, lambda g, o: (0, 0, 0)),
            pl.BlockSpec(weights.shape, lambda g, o: (0, 0)),
            pl.BlockSpec((block, deg_count, half_lats), lambda g, o: (g, 0, 0)),
        ],
        out_specs=pl.BlockSpec((block, epochs, parts, deg_count), lambda g, o: (g, 0, 0, 0)),
    )
    return pl.pallas_call(
        _analysis_kernel,
        grid_spec=grid_spec,
        out_shape=jax.ShapeDtypeStruct((slot_cap, epochs, parts, deg_count), jnp.bfloat16),
        compiler_params=pltpu.CompilerParams(dimension_semantics=("arbitrary",)),
        cost_estimate=pl.CostEstimate(
            flops=2 * slot_cap * 2 * half * deg_count * half_lats,
            bytes_accessed=legendre.size * 2 + returned.size * 2 + slot_cap * half * deg_count * 2,
            transcendentals=0,
        ),
    )(orders, returned, pick, weights, legendre)


def inner_length(lon_count):
    best = 1
    for factor in range(1, math.isqrt(lon_count) + 1):
        if lon_count % factor == 0:
            best = factor
    return best


def one_hot_rows(lat_map, lat_rows):
    return (lat_map[None, :] == jnp.arange(lat_rows, dtype=jnp.int32)[:, None]).astype(jnp.bfloat16)


def angle(numer, denom):
    return jnp.float32(2.0 * math.pi) * (numer % denom).astype(jnp.float32) / jnp.float32(denom)


def transform_blocks(x_parts, lon_count):
    highest = lax.Precision.HIGHEST
    _, outer, blocks, signals = x_parts.shape
    inner = lon_count // outer
    a_idx = jnp.arange(outer, dtype=jnp.int32)
    b_idx = jnp.arange(inner, dtype=jnp.int32)
    c_idx = jnp.arange(blocks, dtype=jnp.int32)
    w1 = angle(b_idx[:, None] * c_idx[None, :], inner)
    w1c, w1s = jnp.cos(w1), jnp.sin(w1)
    tw = angle(b_idx[:, None] * a_idx[None, :], lon_count)
    twc, tws = jnp.cos(tw)[:, :, None], jnp.sin(tw)[:, :, None]
    w2 = angle(a_idx[:, None] * a_idx[None, :], outer)
    w2c, w2s = jnp.cos(w2), jnp.sin(w2)

    def mm(spec, left, right):
        return jnp.einsum(spec, left, right, precision=highest)

    rot1 = jnp.stack([jnp.stack([w1c, -w1s]), jnp.stack([w1s, w1c])])
    y = mm("kjbc,jdcq->kbdq", rot1, x_parts)
    t_re = y[0] * twc - y[1] * tws
    t_im = y[0] * tws + y[1] * twc
    field = mm("jad,jbdq->abq", jnp.stack([w2c, -w2s]), jnp.stack([t_re, t_im]))
    squared = (field * field).astype(jnp.bfloat16)
    sq = squared.astype(jnp.float32)
    z = mm("kda,abq->kbdq", jnp.stack([w2c, -w2s]), sq)
    u_re = z[0] * twc + z[1] * tws
    u_im = z[1] * twc - z[0] * tws
    rot2 = jnp.stack([jnp.stack([w1c, w1s]), jnp.stack([-w1s, w1c])])
    f = mm("kjbc,jbdq->kcdq", rot2, jnp.stack([u_re, u_im]))
    first = (c_idx[:, None] == 0) & (a_idx[None, :] == 0)
    scaling = jnp.where(first, 1.0, 2.0).astype(jnp.float32)[:, :, None] / lon_count
    four_cos = f[0] * scaling
    four_sin = -f[1] * scaling
    grid = jnp.transpose(squared, (2, 0, 1)).reshape(signals, lon_count)
    return grid, four_cos, four_sin


def shards(coeffs, legendre, orders, lat_map, weights):
    slot_cap = coeffs.shape[0]
    epoch_count = coeffs.shape[1]
    deg_count = legendre.shape[1]
    half_lats = legendre.shape[2]
    lon_count = 2 * deg_count
    lat_rows = lat_map.shape[0]
    devices = lax.axis_size(("gx", "gy"))
    rows_each = lat_rows // devices

    synth = synthesize(coeffs, legendre, orders).reshape(slot_cap, 2, epoch_count * 2, half_lats)
    full_lats = jnp.concatenate([synth[:, 0], synth[:, 1, :, ::-1]], axis=-1)

    onehot = one_hot_rows(lat_map, lat_rows)
    permuted = jnp.einsum(
        "sxk,kr->sxr", full_lats, onehot, preferred_element_type=jnp.float32
    ).astype(jnp.bfloat16)
    sends = permuted.reshape(slot_cap, epoch_count * 2, devices, rows_each)
    sends = jnp.transpose(sends, (2, 0, 1, 3)).reshape(devices, slot_cap, epoch_count * 2 * rows_each)
    inner = inner_length(lon_count)
    outer = lon_count // inner
    blocks = deg_count // outer
    block_of = jnp.where(orders >= 0, orders // outer, -1)
    order_code = jnp.stack([block_of, orders % outer], axis=-1).astype(jnp.bfloat16)
    order_code = jnp.broadcast_to(order_code[None], (devices, slot_cap, 2))
    payload = jnp.concatenate([sends, order_code], axis=-1).reshape(devices, -1)
    width = payload.shape[1]
    padded = -(-width // 256) * 256
    payload = jnp.pad(payload, ((0, 0), (0, padded - width))).reshape(devices, padded // 128, 128)
    got = lax.all_to_all(payload, ("gx", "gy"), 0, 0, tiled=True)
    got = got.reshape(devices, padded)[:, :width].reshape(devices * slot_cap, -1)
    data = got[:, :-2]
    by_d = (got[:, -1:] == jnp.arange(outer, dtype=jnp.bfloat16)[None, :]).astype(jnp.bfloat16)
    in_c = got[:, -2:-1] == jnp.arange(blocks, dtype=jnp.bfloat16)[None, :]
    spread = jnp.where(in_c[:, :, None], data[:, None, :], jnp.zeros((), jnp.bfloat16))
    dense = jnp.einsum("sd,scr->dcr", by_d, spread, preferred_element_type=jnp.float32)
    dense = dense.reshape(outer, blocks, epoch_count, 2, rows_each)
    x_parts = jnp.stack([dense[:, :, :, 0, :], -dense[:, :, :, 1, :]])
    x_parts = jnp.transpose(x_parts, (0, 1, 2, 4, 3)).reshape(2, outer, blocks, rows_each * epoch_count)
    grid, four_cos, four_sin = transform_blocks(x_parts, lon_count)
    grid_rows = grid.reshape(rows_each, epoch_count, lon_count)

    split = (blocks, outer, rows_each, epoch_count)
    fourier = jnp.stack([four_cos.reshape(split), four_sin.reshape(split)], axis=4)
    fourier = jnp.transpose(fourier, (0, 1, 3, 4, 2))
    fourier = fourier.astype(jnp.bfloat16).reshape(blocks, outer, -1)
    picked = jnp.einsum("sd,cdr->scr", by_d, fourier, preferred_element_type=jnp.float32)
    by_slot = jnp.sum(jnp.where(in_c[:, :, None], picked, jnp.float32(0.0)), axis=1)
    back = by_slot.astype(jnp.bfloat16).reshape(devices, -1)
    width = back.shape[1]
    padded = -(-width // 256) * 256
    back = jnp.pad(back, ((0, 0), (0, padded - width))).reshape(devices, padded // 128, 128)
    back = lax.all_to_all(back, ("gx", "gy"), 0, 0, tiled=True)
    back = back.reshape(devices, padded)[:, :width].reshape(devices, slot_cap, epoch_count, 2, rows_each)
    returned = jnp.transpose(back, (1, 2, 3, 0, 4)).reshape(slot_cap * epoch_count * 2, lat_rows)
    lat_ids = jnp.arange(half_lats, dtype=jnp.int32)[None, :]
    pick = jnp.stack([lat_map[:, None] == lat_ids, lat_map[:, None] == lat_rows - 1 - lat_ids])
    spectra = analyze(
        returned, pick.astype(jnp.bfloat16), weights.reshape(1, -1), legendre, orders, epoch_count, 2
    )
    return (grid_rows, spectra)


def solution(mesh):
    placed = (
        P(("gx", "gy"), None, None, None),
        P(("gx", "gy"), None, None),
        P(("gx", "gy")),
        P(),
        P(),
    )
    return jax.shard_map(
        shards,
        mesh=mesh,
        in_specs=placed,
        out_specs=(P(("gx", "gy"), None, None), P(("gx", "gy"), None, None, None)),
        check_vma=False,
    )
```

```python
import math

import jax
import jax.numpy as jnp
from jax import lax
from jax.experimental import pallas as pl
from jax.experimental.pallas import tpu as pltpu
from jax.sharding import PartitionSpec as P

ORDER_OUTER = 72

SLOTS_PER_STEP = 12


def _masks(order, deg_count):
    degrees = lax.broadcasted_iota(jnp.int32, (1, deg_count), 1)
    usable = (degrees >= order) & (order >= 0)
    even = ((degrees + order) & 1) == 0
    return usable, even


def _synth_kernel(orders_ref, coef_ref, leg_ref, out_ref):
    step = pl.program_id(0)
    block, epochs, _, deg_count = coef_ref.shape
    zero = jnp.zeros((), coef_ref.dtype)
    for i in range(block):
        order = orders_ref[step * block + i]
        usable, even = _masks(order, deg_count)
        rows = jnp.concatenate([coef_ref[i, e] for e in range(epochs)], axis=0)
        masked = jnp.where(usable, rows, zero)
        signed = jnp.where(even, masked, -masked)
        lhs = jnp.concatenate([masked, signed], axis=0)
        res = jnp.dot(lhs, leg_ref[i], preferred_element_type=jnp.float32)
        held = jnp.full((1, res.shape[1]), order, jnp.int32).astype(jnp.float32)
        block_of = jnp.floor((held + 0.5) / ORDER_OUTER)
        code = jnp.concatenate([block_of, held - ORDER_OUTER * block_of], axis=0)
        out_ref[i] = jnp.concatenate([res, code], axis=0).astype(out_ref.dtype)


def synthesize(coeffs, legendre, orders):
    slot_cap, epochs, parts, deg_count = coeffs.shape
    half_lats = legendre.shape[2]
    block = SLOTS_PER_STEP
    rows = 2 * epochs * parts + 2
    grid_spec = pltpu.PrefetchScalarGridSpec(
        num_scalar_prefetch=1,
        grid=(slot_cap // block,),
        in_specs=[
            pl.BlockSpec((block, epochs, parts, deg_count), lambda g, o: (g, 0, 0, 0)),
            pl.BlockSpec((block, deg_count, half_lats), lambda g, o: (g, 0, 0)),
        ],
        out_specs=pl.BlockSpec((block, rows, half_lats), lambda g, o: (g, 0, 0)),
    )
    return pl.pallas_call(
        _synth_kernel,
        grid_spec=grid_spec,
        out_shape=jax.ShapeDtypeStruct((slot_cap, rows, half_lats), jnp.bfloat16),
        compiler_params=pltpu.CompilerParams(dimension_semantics=("arbitrary",)),
        cost_estimate=pl.CostEstimate(
            flops=2 * slot_cap * rows * deg_count * half_lats,
            bytes_accessed=legendre.size * 2 + coeffs.size * 2 + slot_cap * rows * half_lats * 2,
            transcendentals=0,
        ),
    )(orders, coeffs, legendre)


def _analysis_kernel(orders_ref, both_ref, leg_ref, out_ref):
    step = pl.program_id(0)
    block, epochs, parts, deg_count = out_ref.shape
    half = epochs * parts
    for i in range(block):
        order = orders_ref[step * block + i]
        usable, even = _masks(order, deg_count)
        res = lax.dot_general(
            both_ref[i], leg_ref[i], (((1,), (1,)), ((), ())), preferred_element_type=jnp.float32
        )
        chosen = jnp.where(even, res[:half], res[half:])
        chosen = jnp.where(usable, chosen, jnp.float32(0.0)).astype(out_ref.dtype)
        for e in range(epochs):
            out_ref[i, e] = chosen[e * parts:(e + 1) * parts]


def analyze(both, legendre, orders, epochs, parts):
    slot_cap, rows, half_lats = both.shape
    deg_count = legendre.shape[1]
    block = SLOTS_PER_STEP
    grid_spec = pltpu.PrefetchScalarGridSpec(
        num_scalar_prefetch=1,
        grid=(slot_cap // block,),
        in_specs=[
            pl.BlockSpec((block, rows, half_lats), lambda g, o: (g, 0, 0)),
            pl.BlockSpec((block, deg_count, half_lats), lambda g, o: (g, 0, 0)),
        ],
        out_specs=pl.BlockSpec((block, epochs, parts, deg_count), lambda g, o: (g, 0, 0, 0)),
    )
    return pl.pallas_call(
        _analysis_kernel,
        grid_spec=grid_spec,
        out_shape=jax.ShapeDtypeStruct((slot_cap, epochs, parts, deg_count), jnp.bfloat16),
        compiler_params=pltpu.CompilerParams(dimension_semantics=("arbitrary",)),
        cost_estimate=pl.CostEstimate(
            flops=2 * slot_cap * rows * deg_count * half_lats,
            bytes_accessed=legendre.size * 2 + both.size * 2 + slot_cap * epochs * parts * deg_count * 2,
            transcendentals=0,
        ),
    )(orders, both, legendre)


def inner_length(lon_count):
    best = 1
    for factor in range(1, math.isqrt(lon_count) + 1):
        if lon_count % factor == 0:
            best = factor
    return best


def one_hot_rows(lat_map, lat_rows):
    return (lat_map[None, :] == jnp.arange(lat_rows, dtype=jnp.int32)[:, None]).astype(jnp.bfloat16)


def angle(numer, denom):
    return jnp.float32(2.0 * math.pi) * (numer % denom).astype(jnp.float32) / jnp.float32(denom)


def transform_blocks(x_parts, lon_count):
    highest = lax.Precision.HIGHEST
    _, outer, blocks, signals = x_parts.shape
    inner = lon_count // outer
    a_idx = jnp.arange(outer, dtype=jnp.int32)
    b_idx = jnp.arange(inner, dtype=jnp.int32)
    c_idx = jnp.arange(blocks, dtype=jnp.int32)
    w1 = angle(b_idx[:, None] * c_idx[None, :], inner)
    w1c, w1s = jnp.cos(w1), jnp.sin(w1)
    tw = angle(b_idx[:, None] * a_idx[None, :], lon_count)
    twc, tws = jnp.cos(tw)[:, :, None], jnp.sin(tw)[:, :, None]
    w2 = angle(a_idx[:, None] * a_idx[None, :], outer)
    w2c, w2s = jnp.cos(w2), jnp.sin(w2)

    def mm(spec, left, right):
        return jnp.einsum(spec, left, right, precision=highest)

    rot1 = jnp.stack([jnp.stack([w1c, -w1s]), jnp.stack([w1s, w1c])])
    y = mm("kjbc,jdcq->kbdq", rot1, x_parts)
    t_re = y[0] * twc - y[1] * tws
    t_im = y[0] * tws + y[1] * twc
    field = mm("jad,jbdq->abq", jnp.stack([w2c, -w2s]), jnp.stack([t_re, t_im]))
    squared = (field * field).astype(jnp.bfloat16)
    sq = squared.astype(jnp.float32)
    z = mm("kda,abq->kbdq", jnp.stack([w2c, -w2s]), sq)
    u_re = z[0] * twc + z[1] * tws
    u_im = z[1] * twc - z[0] * tws
    rot2 = jnp.stack([jnp.stack([w1c, w1s]), jnp.stack([-w1s, w1c])])
    f = mm("kjbc,jbdq->kcdq", rot2, jnp.stack([u_re, u_im]))
    first = (c_idx[:, None] == 0) & (a_idx[None, :] == 0)
    scaling = jnp.where(first, 1.0, 2.0).astype(jnp.float32)[:, :, None] / lon_count
    four_cos = f[0] * scaling
    four_sin = -f[1] * scaling
    grid = jnp.transpose(squared, (2, 0, 1)).reshape(signals, lon_count)
    return grid, four_cos, four_sin


def shards(coeffs, legendre, orders, lat_map, weights):
    slot_cap = coeffs.shape[0]
    epoch_count = coeffs.shape[1]
    deg_count = legendre.shape[1]
    half_lats = legendre.shape[2]
    lon_count = 2 * deg_count
    lat_rows = lat_map.shape[0]
    devices = lax.axis_size(("gx", "gy"))
    rows_each = lat_rows // devices

    synth_out = synthesize(coeffs, legendre, orders)
    synth = synth_out[:, :-2].reshape(slot_cap, 2, epoch_count * 2, half_lats)
    full_lats = jnp.concatenate([synth[:, 0], synth[:, 1, :, ::-1]], axis=-1)

    onehot = one_hot_rows(lat_map, lat_rows)
    permuted = jnp.einsum(
        "sxk,kr->sxr", full_lats, onehot, preferred_element_type=jnp.float32
    ).astype(jnp.bfloat16)
    sends = permuted.reshape(slot_cap, epoch_count * 2, devices, rows_each)
    sends = jnp.transpose(sends, (2, 0, 1, 3)).reshape(devices, slot_cap, epoch_count * 2 * rows_each)
    inner = inner_length(lon_count)
    outer = lon_count // inner
    blocks = deg_count // outer
    assert outer == ORDER_OUTER
    order_code = synth_out[:, -2:, 0]
    order_code = jnp.broadcast_to(order_code[None], (devices, slot_cap, 2))
    payload = jnp.concatenate([sends, order_code], axis=-1).reshape(devices, -1)
    width = payload.shape[1]
    padded = -(-width // 256) * 256
    payload = jnp.pad(payload, ((0, 0), (0, padded - width))).reshape(devices, padded // 128, 128)
    got = lax.all_to_all(payload, ("gx", "gy"), 0, 0, tiled=True)
    got = got.reshape(devices, padded)[:, :width].reshape(devices * slot_cap, -1)
    data = got[:, :-2]
    by_d = (got[:, -1:] == jnp.arange(outer, dtype=jnp.bfloat16)[None, :]).astype(jnp.bfloat16)
    in_c = got[:, -2:-1] == jnp.arange(blocks, dtype=jnp.bfloat16)[None, :]
    spread = jnp.where(in_c[:, :, None], data[:, None, :], jnp.zeros((), jnp.bfloat16))
    dense = jnp.einsum("sd,scr->dcr", by_d, spread, preferred_element_type=jnp.float32)
    dense = dense.reshape(outer, blocks, epoch_count, 2, rows_each)
    x_parts = jnp.stack([dense[:, :, :, 0, :], -dense[:, :, :, 1, :]])
    x_parts = jnp.transpose(x_parts, (0, 1, 2, 4, 3)).reshape(2, outer, blocks, rows_each * epoch_count)
    grid, four_cos, four_sin = transform_blocks(x_parts, lon_count)
    grid_rows = grid.reshape(rows_each, epoch_count, lon_count)

    split = (blocks, outer, rows_each, epoch_count)
    fourier = jnp.stack([four_cos.reshape(split), four_sin.reshape(split)], axis=4)
    fourier = jnp.transpose(fourier, (0, 1, 3, 4, 2))
    fourier = fourier.astype(jnp.bfloat16).reshape(blocks, outer, -1)
    picked = jnp.einsum("sd,cdr->scr", by_d, fourier, preferred_element_type=jnp.float32)
    by_slot = jnp.sum(jnp.where(in_c[:, :, None], picked, jnp.float32(0.0)), axis=1)
    back = by_slot.astype(jnp.bfloat16).reshape(devices, -1)
    width = back.shape[1]
    padded = -(-width // 256) * 256
    back = jnp.pad(back, ((0, 0), (0, padded - width))).reshape(devices, padded // 128, 128)
    back = lax.all_to_all(back, ("gx", "gy"), 0, 0, tiled=True)
    back = back.reshape(devices, padded)[:, :width].reshape(devices, slot_cap, epoch_count, 2, rows_each)
    returned = jnp.transpose(back, (1, 2, 3, 0, 4)).reshape(slot_cap, epoch_count * 2, lat_rows)
    natural = jnp.einsum(
        "sxr,kr->sxk", returned, onehot, preferred_element_type=jnp.float32
    )
    northern = natural[..., :half_lats]
    southern = natural[..., half_lats:][..., ::-1]
    sym_part = ((northern + southern) * weights).astype(jnp.bfloat16)
    anti_part = ((northern - southern) * weights).astype(jnp.bfloat16)
    both = jnp.concatenate([sym_part, anti_part], axis=1)
    spectra = analyze(both, legendre, orders, epoch_count, 2)
    return (grid_rows, spectra)


def solution(mesh):
    placed = (
        P(("gx", "gy"), None, None, None),
        P(("gx", "gy"), None, None),
        P(("gx", "gy")),
        P(),
        P(),
    )
    return jax.shard_map(
        shards,
        mesh=mesh,
        in_specs=placed,
        out_specs=(P(("gx", "gy"), None, None), P(("gx", "gy"), None, None, None)),
        check_vma=False,
    )
```

```python
import math

import jax
import jax.numpy as jnp
from jax import lax
from jax.experimental import pallas as pl
from jax.experimental.pallas import tpu as pltpu
from jax.sharding import PartitionSpec as P

ORDER_OUTER = 72

SLOTS_PER_STEP = 12


def _masks(order, deg_count):
    degrees = lax.broadcasted_iota(jnp.int32, (1, deg_count), 1)
    usable = (degrees >= order) & (order >= 0)
    even = ((degrees + order) & 1) == 0
    return usable, even


def _synth_kernel(orders_ref, coef_ref, leg_ref, out_ref, code_ref):
    step = pl.program_id(0)
    block, epochs, _, deg_count = coef_ref.shape
    zero = jnp.zeros((), coef_ref.dtype)
    for i in range(block):
        order = orders_ref[step * block + i]
        usable, even = _masks(order, deg_count)
        rows = jnp.concatenate([coef_ref[i, e] for e in range(epochs)], axis=0)
        masked = jnp.where(usable, rows, zero)
        signed = jnp.where(even, masked, -masked)
        lhs = jnp.concatenate([masked, signed], axis=0)
        res = jnp.dot(lhs, leg_ref[i], preferred_element_type=jnp.float32)
        held = jnp.full((1, res.shape[1]), order, jnp.int32).astype(jnp.float32)
        block_of = jnp.floor((held + 0.5) / ORDER_OUTER)
        code = jnp.concatenate([block_of, held - ORDER_OUTER * block_of], axis=0)
        out_ref[i] = res.astype(out_ref.dtype)
        code_ref[i] = code.astype(code_ref.dtype)


def synthesize(coeffs, legendre, orders):
    slot_cap, epochs, parts, deg_count = coeffs.shape
    half_lats = legendre.shape[2]
    block = SLOTS_PER_STEP
    rows = 2 * epochs * parts
    grid_spec = pltpu.PrefetchScalarGridSpec(
        num_scalar_prefetch=1,
        grid=(slot_cap // block,),
        in_specs=[
            pl.BlockSpec((block, epochs, parts, deg_count), lambda g, o: (g, 0, 0, 0)),
            pl.BlockSpec((block, deg_count, half_lats), lambda g, o: (g, 0, 0)),
        ],
        out_specs=[
            pl.BlockSpec((block, rows, half_lats), lambda g, o: (g, 0, 0)),
            pl.BlockSpec((block, 2, half_lats), lambda g, o: (g, 0, 0)),
        ],
    )
    return pl.pallas_call(
        _synth_kernel,
        grid_spec=grid_spec,
        out_shape=[
            jax.ShapeDtypeStruct((slot_cap, rows, half_lats), jnp.bfloat16),
            jax.ShapeDtypeStruct((slot_cap, 2, half_lats), jnp.bfloat16),
        ],
        compiler_params=pltpu.CompilerParams(dimension_semantics=("arbitrary",)),
        cost_estimate=pl.CostEstimate(
            flops=2 * slot_cap * rows * deg_count * half_lats,
            bytes_accessed=legendre.size * 2 + coeffs.size * 2 + slot_cap * rows * half_lats * 2,
            transcendentals=0,
        ),
    )(orders, coeffs, legendre)


def _analysis_kernel(orders_ref, both_ref, leg_ref, out_ref):
    step = pl.program_id(0)
    block, epochs, parts, deg_count = out_ref.shape
    half = epochs * parts
    for i in range(block):
        order = orders_ref[step * block + i]
        usable, even = _masks(order, deg_count)
        res = lax.dot_general(
            both_ref[i], leg_ref[i], (((1,), (1,)), ((), ())), preferred_element_type=jnp.float32
        )
        chosen = jnp.where(even, res[:half], res[half:])
        chosen = jnp.where(usable, chosen, jnp.float32(0.0)).astype(out_ref.dtype)
        for e in range(epochs):
            out_ref[i, e] = chosen[e * parts:(e + 1) * parts]


def analyze(both, legendre, orders, epochs, parts):
    slot_cap, rows, half_lats = both.shape
    deg_count = legendre.shape[1]
    block = SLOTS_PER_STEP
    grid_spec = pltpu.PrefetchScalarGridSpec(
        num_scalar_prefetch=1,
        grid=(slot_cap // block,),
        in_specs=[
            pl.BlockSpec((block, rows, half_lats), lambda g, o: (g, 0, 0)),
            pl.BlockSpec((block, deg_count, half_lats), lambda g, o: (g, 0, 0)),
        ],
        out_specs=pl.BlockSpec((block, epochs, parts, deg_count), lambda g, o: (g, 0, 0, 0)),
    )
    return pl.pallas_call(
        _analysis_kernel,
        grid_spec=grid_spec,
        out_shape=jax.ShapeDtypeStruct((slot_cap, epochs, parts, deg_count), jnp.bfloat16),
        compiler_params=pltpu.CompilerParams(dimension_semantics=("arbitrary",)),
        cost_estimate=pl.CostEstimate(
            flops=2 * slot_cap * rows * deg_count * half_lats,
            bytes_accessed=legendre.size * 2 + both.size * 2 + slot_cap * epochs * parts * deg_count * 2,
            transcendentals=0,
        ),
    )(orders, both, legendre)


def inner_length(lon_count):
    best = 1
    for factor in range(1, math.isqrt(lon_count) + 1):
        if lon_count % factor == 0:
            best = factor
    return best


def one_hot_rows(lat_map, lat_rows):
    return (lat_map[None, :] == jnp.arange(lat_rows, dtype=jnp.int32)[:, None]).astype(jnp.bfloat16)


def angle(numer, denom):
    return jnp.float32(2.0 * math.pi) * (numer % denom).astype(jnp.float32) / jnp.float32(denom)


def transform_blocks(x_parts, lon_count):
    highest = lax.Precision.HIGHEST
    _, outer, blocks, signals = x_parts.shape
    inner = lon_count // outer
    a_idx = jnp.arange(outer, dtype=jnp.int32)
    b_idx = jnp.arange(inner, dtype=jnp.int32)
    c_idx = jnp.arange(blocks, dtype=jnp.int32)
    w1 = angle(b_idx[:, None] * c_idx[None, :], inner)
    w1c, w1s = jnp.cos(w1), jnp.sin(w1)
    tw = angle(b_idx[:, None] * a_idx[None, :], lon_count)
    twc, tws = jnp.cos(tw)[:, :, None], jnp.sin(tw)[:, :, None]
    w2 = angle(a_idx[:, None] * a_idx[None, :], outer)
    w2c, w2s = jnp.cos(w2), jnp.sin(w2)

    def mm(spec, left, right):
        return jnp.einsum(spec, left, right, precision=highest)

    rot1 = jnp.stack([jnp.stack([w1c, -w1s]), jnp.stack([w1s, w1c])])
    y = mm("kjbc,jdcq->kbdq", rot1, x_parts)
    t_re = y[0] * twc - y[1] * tws
    t_im = y[0] * tws + y[1] * twc
    field = mm("jad,jbdq->abq", jnp.stack([w2c, -w2s]), jnp.stack([t_re, t_im]))
    squared = (field * field).astype(jnp.bfloat16)
    sq = squared.astype(jnp.float32)
    z = mm("kda,abq->kbdq", jnp.stack([w2c, -w2s]), sq)
    u_re = z[0] * twc + z[1] * tws
    u_im = z[1] * twc - z[0] * tws
    rot2 = jnp.stack([jnp.stack([w1c, w1s]), jnp.stack([-w1s, w1c])])
    f = mm("kjbc,jbdq->kcdq", rot2, jnp.stack([u_re, u_im]))
    first = (c_idx[:, None] == 0) & (a_idx[None, :] == 0)
    scaling = jnp.where(first, 1.0, 2.0).astype(jnp.float32)[:, :, None] / lon_count
    four_cos = f[0] * scaling
    four_sin = -f[1] * scaling
    grid = jnp.transpose(squared, (2, 0, 1)).reshape(signals, lon_count)
    return grid, four_cos, four_sin


def shards(coeffs, legendre, orders, lat_map, weights):
    slot_cap = coeffs.shape[0]
    epoch_count = coeffs.shape[1]
    deg_count = legendre.shape[1]
    half_lats = legendre.shape[2]
    lon_count = 2 * deg_count
    lat_rows = lat_map.shape[0]
    devices = lax.axis_size(("gx", "gy"))
    rows_each = lat_rows // devices

    synth, codes = synthesize(coeffs, legendre, orders)
    synth = synth.reshape(slot_cap, 2, epoch_count * 2, half_lats)
    full_lats = jnp.concatenate([synth[:, 0], synth[:, 1, :, ::-1]], axis=-1)

    onehot = one_hot_rows(lat_map, lat_rows)
    permuted = jnp.einsum(
        "sxk,kr->sxr", full_lats, onehot, preferred_element_type=jnp.float32
    ).astype(jnp.bfloat16)
    sends = permuted.reshape(slot_cap, epoch_count * 2, devices, rows_each)
    sends = jnp.transpose(sends, (2, 0, 1, 3)).reshape(devices, slot_cap, epoch_count * 2 * rows_each)
    inner = inner_length(lon_count)
    outer = lon_count // inner
    blocks = deg_count // outer
    assert outer == ORDER_OUTER
    order_code = codes[:, :, 0]
    order_code = jnp.broadcast_to(order_code[None], (devices, slot_cap, 2))
    payload = jnp.concatenate([sends, order_code], axis=-1).reshape(devices, -1)
    width = payload.shape[1]
    padded = -(-width // 256) * 256
    payload = jnp.pad(payload, ((0, 0), (0, padded - width))).reshape(devices, padded // 128, 128)
    got = lax.all_to_all(payload, ("gx", "gy"), 0, 0, tiled=True)
    got = got.reshape(devices, padded)[:, :width].reshape(devices * slot_cap, -1)
    data = got[:, :-2]
    by_d = (got[:, -1:] == jnp.arange(outer, dtype=jnp.bfloat16)[None, :]).astype(jnp.bfloat16)
    in_c = got[:, -2:-1] == jnp.arange(blocks, dtype=jnp.bfloat16)[None, :]
    spread = jnp.where(in_c[:, :, None], data[:, None, :], jnp.zeros((), jnp.bfloat16))
    dense = jnp.einsum("sd,scr->dcr", by_d, spread, preferred_element_type=jnp.float32)
    dense = dense.reshape(outer, blocks, epoch_count, 2, rows_each)
    x_parts = jnp.stack([dense[:, :, :, 0, :], -dense[:, :, :, 1, :]])
    x_parts = jnp.transpose(x_parts, (0, 1, 2, 4, 3)).reshape(2, outer, blocks, rows_each * epoch_count)
    grid, four_cos, four_sin = transform_blocks(x_parts, lon_count)
    grid_rows = grid.reshape(rows_each, epoch_count, lon_count)

    split = (blocks, outer, rows_each, epoch_count)
    fourier = jnp.stack([four_cos.reshape(split), four_sin.reshape(split)], axis=4)
    fourier = jnp.transpose(fourier, (0, 1, 3, 4, 2))
    fourier = fourier.astype(jnp.bfloat16).reshape(blocks, outer, -1)
    picked = jnp.einsum("sd,cdr->scr", by_d, fourier, preferred_element_type=jnp.float32)
    by_slot = jnp.sum(jnp.where(in_c[:, :, None], picked, jnp.float32(0.0)), axis=1)
    back = by_slot.astype(jnp.bfloat16).reshape(devices, -1)
    width = back.shape[1]
    padded = -(-width // 256) * 256
    back = jnp.pad(back, ((0, 0), (0, padded - width))).reshape(devices, padded // 128, 128)
    back = lax.all_to_all(back, ("gx", "gy"), 0, 0, tiled=True)
    back = back.reshape(devices, padded)[:, :width].reshape(devices, slot_cap, epoch_count, 2, rows_each)
    returned = jnp.transpose(back, (1, 2, 3, 0, 4)).reshape(slot_cap, epoch_count * 2, lat_rows)
    natural = jnp.einsum(
        "sxr,kr->sxk", returned, onehot, preferred_element_type=jnp.float32
    )
    northern = natural[..., :half_lats]
    southern = natural[..., half_lats:][..., ::-1]
    sym_part = ((northern + southern) * weights).astype(jnp.bfloat16)
    anti_part = ((northern - southern) * weights).astype(jnp.bfloat16)
    both = jnp.concatenate([sym_part, anti_part], axis=1)
    spectra = analyze(both, legendre, orders, epoch_count, 2)
    return (grid_rows, spectra)


def solution(mesh):
    placed = (
        P(("gx", "gy"), None, None, None),
        P(("gx", "gy"), None, None),
        P(("gx", "gy")),
        P(),
        P(),
    )
    return jax.shard_map(
        shards,
        mesh=mesh,
        in_specs=placed,
        out_specs=(P(("gx", "gy"), None, None), P(("gx", "gy"), None, None, None)),
        check_vma=False,
    )
```

```python
import math

import jax
import jax.numpy as jnp
from jax import lax
from jax.experimental import pallas as pl
from jax.experimental.pallas import tpu as pltpu
from jax.sharding import PartitionSpec as P


SLOTS_PER_STEP = 12


def _masks(order, deg_count):
    degrees = lax.broadcasted_iota(jnp.int32, (1, deg_count), 1)
    usable = (degrees >= order) & (order >= 0)
    even = ((degrees + order) & 1) == 0
    return usable, even


def _synth_kernel(orders_ref, coef_ref, leg_ref, out_ref):
    step = pl.program_id(0)
    block, epochs, _, deg_count = coef_ref.shape
    zero = jnp.zeros((), coef_ref.dtype)
    for i in range(block):
        order = orders_ref[step * block + i]
        usable, even = _masks(order, deg_count)
        rows = jnp.concatenate([coef_ref[i, e] for e in range(epochs)], axis=0)
        masked = jnp.where(usable, rows, zero)
        signed = jnp.where(even, masked, -masked)
        lhs = jnp.concatenate([masked, signed], axis=0)
        out_ref[i] = jnp.dot(lhs, leg_ref[i], preferred_element_type=jnp.float32).astype(out_ref.dtype)


def synthesize(coeffs, legendre, orders):
    slot_cap, epochs, parts, deg_count = coeffs.shape
    half_lats = legendre.shape[2]
    block = SLOTS_PER_STEP
    rows = 2 * epochs * parts
    grid_spec = pltpu.PrefetchScalarGridSpec(
        num_scalar_prefetch=1,
        grid=(slot_cap // block,),
        in_specs=[
            pl.BlockSpec((block, epochs, parts, deg_count), lambda g, o: (g, 0, 0, 0)),
            pl.BlockSpec((block, deg_count, half_lats), lambda g, o: (g, 0, 0)),
        ],
        out_specs=pl.BlockSpec((block, rows, half_lats), lambda g, o: (g, 0, 0)),
    )
    return pl.pallas_call(
        _synth_kernel,
        grid_spec=grid_spec,
        out_shape=jax.ShapeDtypeStruct((slot_cap, rows, half_lats), jnp.bfloat16),
        compiler_params=pltpu.CompilerParams(dimension_semantics=("arbitrary",)),
        cost_estimate=pl.CostEstimate(
            flops=2 * slot_cap * rows * deg_count * half_lats,
            bytes_accessed=legendre.size * 2 + coeffs.size * 2 + slot_cap * rows * half_lats * 2,
            transcendentals=0,
        ),
    )(orders, coeffs, legendre)


def _analysis_kernel(orders_ref, both_ref, leg_ref, out_ref):
    step = pl.program_id(0)
    block, epochs, parts, deg_count = out_ref.shape
    half = epochs * parts
    for i in range(block):
        order = orders_ref[step * block + i]
        usable, even = _masks(order, deg_count)
        res = lax.dot_general(
            both_ref[i], leg_ref[i], (((1,), (1,)), ((), ())), preferred_element_type=jnp.float32
        )
        chosen = jnp.where(even, res[:half], res[half:])
        chosen = jnp.where(usable, chosen, jnp.float32(0.0)).astype(out_ref.dtype)
        for e in range(epochs):
            out_ref[i, e] = chosen[e * parts:(e + 1) * parts]


def analyze(both, legendre, orders, epochs, parts):
    slot_cap, rows, half_lats = both.shape
    deg_count = legendre.shape[1]
    block = SLOTS_PER_STEP
    grid_spec = pltpu.PrefetchScalarGridSpec(
        num_scalar_prefetch=1,
        grid=(slot_cap // block,),
        in_specs=[
            pl.BlockSpec((block, rows, half_lats), lambda g, o: (g, 0, 0)),
            pl.BlockSpec((block, deg_count, half_lats), lambda g, o: (g, 0, 0)),
        ],
        out_specs=pl.BlockSpec((block, epochs, parts, deg_count), lambda g, o: (g, 0, 0, 0)),
    )
    return pl.pallas_call(
        _analysis_kernel,
        grid_spec=grid_spec,
        out_shape=jax.ShapeDtypeStruct((slot_cap, epochs, parts, deg_count), jnp.bfloat16),
        compiler_params=pltpu.CompilerParams(dimension_semantics=("arbitrary",)),
        cost_estimate=pl.CostEstimate(
            flops=2 * slot_cap * rows * deg_count * half_lats,
            bytes_accessed=legendre.size * 2 + both.size * 2 + slot_cap * epochs * parts * deg_count * 2,
            transcendentals=0,
        ),
    )(orders, both, legendre)


def inner_length(lon_count):
    best = 1
    for factor in range(1, math.isqrt(lon_count) + 1):
        if lon_count % factor == 0:
            best = factor
    return best


def one_hot_rows(lat_map, lat_rows):
    return (lat_map[None, :] == jnp.arange(lat_rows, dtype=jnp.int32)[:, None]).astype(jnp.bfloat16)


def angle(numer, denom):
    return jnp.float32(2.0 * math.pi) * (numer % denom).astype(jnp.float32) / jnp.float32(denom)


def transform_blocks(x_parts, lon_count):
    highest = lax.Precision.HIGH
    _, outer, blocks, signals = x_parts.shape
    inner = lon_count // outer
    a_idx = jnp.arange(outer, dtype=jnp.int32)
    b_idx = jnp.arange(inner, dtype=jnp.int32)
    c_idx = jnp.arange(blocks, dtype=jnp.int32)
    w1 = angle(b_idx[:, None] * c_idx[None, :], inner)
    w1c, w1s = jnp.cos(w1), jnp.sin(w1)
    tw = angle(b_idx[:, None] * a_idx[None, :], lon_count)
    twc, tws = jnp.cos(tw)[:, :, None], jnp.sin(tw)[:, :, None]
    w2 = angle(a_idx[:, None] * a_idx[None, :], outer)
    w2c, w2s = jnp.cos(w2), jnp.sin(w2)

    def mm(spec, left, right):
        return jnp.einsum(spec, left, right, precision=highest)

    rot1 = jnp.stack([jnp.stack([w1c, -w1s]), jnp.stack([w1s, w1c])])
    y = mm("kjbc,jdcq->kbdq", rot1, x_parts)
    t_re = y[0] * twc - y[1] * tws
    t_im = y[0] * tws + y[1] * twc
    field = mm("jad,jbdq->abq", jnp.stack([w2c, -w2s]), jnp.stack([t_re, t_im]))
    squared = (field * field).astype(jnp.bfloat16)
    sq = squared.astype(jnp.float32)
    z = mm("kda,abq->kbdq", jnp.stack([w2c, -w2s]), sq)
    u_re = z[0] * twc + z[1] * tws
    u_im = z[1] * twc - z[0] * tws
    rot2 = jnp.stack([jnp.stack([w1c, w1s]), jnp.stack([-w1s, w1c])])
    f = mm("kjbc,jbdq->kcdq", rot2, jnp.stack([u_re, u_im]))
    first = (c_idx[:, None] == 0) & (a_idx[None, :] == 0)
    scaling = jnp.where(first, 1.0, 2.0).astype(jnp.float32)[:, :, None] / lon_count
    four_cos = f[0] * scaling
    four_sin = -f[1] * scaling
    grid = jnp.transpose(squared, (2, 0, 1)).reshape(signals, lon_count)
    return grid, four_cos, four_sin


def shards(coeffs, legendre, orders, lat_map, weights):
    slot_cap = coeffs.shape[0]
    epoch_count = coeffs.shape[1]
    deg_count = legendre.shape[1]
    half_lats = legendre.shape[2]
    lon_count = 2 * deg_count
    lat_rows = lat_map.shape[0]
    devices = lax.axis_size(("gx", "gy"))
    rows_each = lat_rows // devices

    synth = synthesize(coeffs, legendre, orders).reshape(slot_cap, 2, epoch_count * 2, half_lats)
    full_lats = jnp.concatenate([synth[:, 0], synth[:, 1, :, ::-1]], axis=-1)

    onehot = one_hot_rows(lat_map, lat_rows)
    permuted = jnp.einsum(
        "sxk,kr->sxr", full_lats, onehot, preferred_element_type=jnp.float32
    ).astype(jnp.bfloat16)
    sends = permuted.reshape(slot_cap, epoch_count * 2, devices, rows_each)
    sends = jnp.transpose(sends, (2, 0, 1, 3)).reshape(devices, slot_cap, epoch_count * 2 * rows_each)
    inner = inner_length(lon_count)
    outer = lon_count // inner
    blocks = deg_count // outer
    block_of = jnp.where(orders >= 0, orders // outer, -1)
    order_code = jnp.stack([block_of, orders % outer], axis=-1).astype(jnp.bfloat16)
    order_code = jnp.broadcast_to(order_code[None], (devices, slot_cap, 2))
    payload = jnp.concatenate([sends, order_code], axis=-1).reshape(devices, -1)
    width = payload.shape[1]
    padded = -(-width // 256) * 256
    payload = jnp.pad(payload, ((0, 0), (0, padded - width))).reshape(devices, padded // 128, 128)
    got = lax.all_to_all(payload, ("gx", "gy"), 0, 0, tiled=True)
    got = got.reshape(devices, padded)[:, :width].reshape(devices * slot_cap, -1)
    data = got[:, :-2]
    by_d = (got[:, -1:] == jnp.arange(outer, dtype=jnp.bfloat16)[None, :]).astype(jnp.bfloat16)
    in_c = got[:, -2:-1] == jnp.arange(blocks, dtype=jnp.bfloat16)[None, :]
    spread = jnp.where(in_c[:, :, None], data[:, None, :], jnp.zeros((), jnp.bfloat16))
    dense = jnp.einsum("sd,scr->dcr", by_d, spread, preferred_element_type=jnp.float32)
    dense = dense.reshape(outer, blocks, epoch_count, 2, rows_each)
    x_parts = jnp.stack([dense[:, :, :, 0, :], -dense[:, :, :, 1, :]])
    x_parts = jnp.transpose(x_parts, (0, 1, 2, 4, 3)).reshape(2, outer, blocks, rows_each * epoch_count)
    grid, four_cos, four_sin = transform_blocks(x_parts, lon_count)
    grid_rows = grid.reshape(rows_each, epoch_count, lon_count)

    split = (blocks, outer, rows_each, epoch_count)
    fourier = jnp.stack([four_cos.reshape(split), four_sin.reshape(split)], axis=4)
    fourier = jnp.transpose(fourier, (0, 1, 3, 4, 2))
    fourier = fourier.astype(jnp.bfloat16).reshape(blocks, outer, -1)
    picked = jnp.einsum("sd,cdr->scr", by_d, fourier, preferred_element_type=jnp.float32)
    by_slot = jnp.sum(jnp.where(in_c[:, :, None], picked, jnp.float32(0.0)), axis=1)
    back = by_slot.astype(jnp.bfloat16).reshape(devices, -1)
    width = back.shape[1]
    padded = -(-width // 256) * 256
    back = jnp.pad(back, ((0, 0), (0, padded - width))).reshape(devices, padded // 128, 128)
    back = lax.all_to_all(back, ("gx", "gy"), 0, 0, tiled=True)
    back = back.reshape(devices, padded)[:, :width].reshape(devices, slot_cap, epoch_count, 2, rows_each)
    returned = jnp.transpose(back, (1, 2, 3, 0, 4)).reshape(slot_cap, epoch_count * 2, lat_rows)
    natural = jnp.einsum(
        "sxr,kr->sxk", returned, onehot, preferred_element_type=jnp.float32
    )
    northern = natural[..., :half_lats]
    southern = natural[..., half_lats:][..., ::-1]
    sym_part = ((northern + southern) * weights).astype(jnp.bfloat16)
    anti_part = ((northern - southern) * weights).astype(jnp.bfloat16)
    both = jnp.concatenate([sym_part, anti_part], axis=1)
    spectra = analyze(both, legendre, orders, epoch_count, 2)
    return (grid_rows, spectra)


def solution(mesh):
    placed = (
        P(("gx", "gy"), None, None, None),
        P(("gx", "gy"), None, None),
        P(("gx", "gy")),
        P(),
        P(),
    )
    return jax.shard_map(
        shards,
        mesh=mesh,
        in_specs=placed,
        out_specs=(P(("gx", "gy"), None, None), P(("gx", "gy"), None, None, None)),
        check_vma=False,
    )
```

```python
import math

import jax
import jax.numpy as jnp
from jax import lax
from jax.experimental import pallas as pl
from jax.experimental.pallas import tpu as pltpu
from jax.sharding import PartitionSpec as P


SLOTS_PER_STEP = 12


def _masks(order, deg_count):
    degrees = lax.broadcasted_iota(jnp.int32, (1, deg_count), 1)
    usable = (degrees >= order) & (order >= 0)
    even = ((degrees + order) & 1) == 0
    return usable, even


def _synth_kernel(orders_ref, coef_ref, leg_ref, out_ref):
    step = pl.program_id(0)
    block, epochs, _, deg_count = coef_ref.shape
    zero = jnp.zeros((), coef_ref.dtype)
    for i in range(block):
        order = orders_ref[step * block + i]
        usable, even = _masks(order, deg_count)
        rows = jnp.concatenate([coef_ref[i, e] for e in range(epochs)], axis=0)
        masked = jnp.where(usable, rows, zero)
        signed = jnp.where(even, masked, -masked)
        lhs = jnp.concatenate([masked, signed], axis=0)
        out_ref[i] = jnp.dot(lhs, leg_ref[i], preferred_element_type=jnp.float32).astype(out_ref.dtype)


def synthesize(coeffs, legendre, orders):
    slot_cap, epochs, parts, deg_count = coeffs.shape
    half_lats = legendre.shape[2]
    block = SLOTS_PER_STEP
    rows = 2 * epochs * parts
    grid_spec = pltpu.PrefetchScalarGridSpec(
        num_scalar_prefetch=1,
        grid=(slot_cap // block,),
        in_specs=[
            pl.BlockSpec((block, epochs, parts, deg_count), lambda g, o: (g, 0, 0, 0)),
            pl.BlockSpec((block, deg_count, half_lats), lambda g, o: (g, 0, 0)),
        ],
        out_specs=pl.BlockSpec((block, rows, half_lats), lambda g, o: (g, 0, 0)),
    )
    return pl.pallas_call(
        _synth_kernel,
        grid_spec=grid_spec,
        out_shape=jax.ShapeDtypeStruct((slot_cap, rows, half_lats), jnp.bfloat16),
        compiler_params=pltpu.CompilerParams(dimension_semantics=("arbitrary",)),
        cost_estimate=pl.CostEstimate(
            flops=2 * slot_cap * rows * deg_count * half_lats,
            bytes_accessed=legendre.size * 2 + coeffs.size * 2 + slot_cap * rows * half_lats * 2,
            transcendentals=0,
        ),
    )(orders, coeffs, legendre)


def _analysis_kernel(orders_ref, both_ref, leg_ref, out_ref):
    step = pl.program_id(0)
    block, epochs, parts, deg_count = out_ref.shape
    half = epochs * parts
    for i in range(block):
        order = orders_ref[step * block + i]
        usable, even = _masks(order, deg_count)
        res = lax.dot_general(
            both_ref[i], leg_ref[i], (((1,), (1,)), ((), ())), preferred_element_type=jnp.float32
        )
        chosen = jnp.where(even, res[:half], res[half:])
        chosen = jnp.where(usable, chosen, jnp.float32(0.0)).astype(out_ref.dtype)
        for e in range(epochs):
            out_ref[i, e] = chosen[e * parts:(e + 1) * parts]


def analyze(both, legendre, orders, epochs, parts):
    slot_cap, rows, half_lats = both.shape
    deg_count = legendre.shape[1]
    block = SLOTS_PER_STEP
    grid_spec = pltpu.PrefetchScalarGridSpec(
        num_scalar_prefetch=1,
        grid=(slot_cap // block,),
        in_specs=[
            pl.BlockSpec((block, rows, half_lats), lambda g, o: (g, 0, 0)),
            pl.BlockSpec((block, deg_count, half_lats), lambda g, o: (g, 0, 0)),
        ],
        out_specs=pl.BlockSpec((block, epochs, parts, deg_count), lambda g, o: (g, 0, 0, 0)),
    )
    return pl.pallas_call(
        _analysis_kernel,
        grid_spec=grid_spec,
        out_shape=jax.ShapeDtypeStruct((slot_cap, epochs, parts, deg_count), jnp.bfloat16),
        compiler_params=pltpu.CompilerParams(dimension_semantics=("arbitrary",)),
        cost_estimate=pl.CostEstimate(
            flops=2 * slot_cap * rows * deg_count * half_lats,
            bytes_accessed=legendre.size * 2 + both.size * 2 + slot_cap * epochs * parts * deg_count * 2,
            transcendentals=0,
        ),
    )(orders, both, legendre)


def inner_length(lon_count):
    best = 1
    for factor in range(1, math.isqrt(lon_count) + 1):
        if lon_count % factor == 0:
            best = factor
    return best


def one_hot_rows(lat_map, lat_rows):
    return (lat_map[None, :] == jnp.arange(lat_rows, dtype=jnp.int32)[:, None]).astype(jnp.bfloat16)


def angle(numer, denom):
    return jnp.float32(2.0 * math.pi) * (numer % denom).astype(jnp.float32) / jnp.float32(denom)


def transform_blocks(x_parts, lon_count):
    highest = lax.Precision.DEFAULT
    _, outer, blocks, signals = x_parts.shape
    inner = lon_count // outer
    a_idx = jnp.arange(outer, dtype=jnp.int32)
    b_idx = jnp.arange(inner, dtype=jnp.int32)
    c_idx = jnp.arange(blocks, dtype=jnp.int32)
    w1 = angle(b_idx[:, None] * c_idx[None, :], inner)
    w1c, w1s = jnp.cos(w1), jnp.sin(w1)
    tw = angle(b_idx[:, None] * a_idx[None, :], lon_count)
    twc, tws = jnp.cos(tw)[:, :, None], jnp.sin(tw)[:, :, None]
    w2 = angle(a_idx[:, None] * a_idx[None, :], outer)
    w2c, w2s = jnp.cos(w2), jnp.sin(w2)

    def mm(spec, left, right):
        return jnp.einsum(spec, left, right, precision=highest)

    rot1 = jnp.stack([jnp.stack([w1c, -w1s]), jnp.stack([w1s, w1c])])
    y = mm("kjbc,jdcq->kbdq", rot1, x_parts)
    t_re = y[0] * twc - y[1] * tws
    t_im = y[0] * tws + y[1] * twc
    field = mm("jad,jbdq->abq", jnp.stack([w2c, -w2s]), jnp.stack([t_re, t_im]))
    squared = (field * field).astype(jnp.bfloat16)
    sq = squared.astype(jnp.float32)
    z = mm("kda,abq->kbdq", jnp.stack([w2c, -w2s]), sq)
    u_re = z[0] * twc + z[1] * tws
    u_im = z[1] * twc - z[0] * tws
    rot2 = jnp.stack([jnp.stack([w1c, w1s]), jnp.stack([-w1s, w1c])])
    f = mm("kjbc,jbdq->kcdq", rot2, jnp.stack([u_re, u_im]))
    first = (c_idx[:, None] == 0) & (a_idx[None, :] == 0)
    scaling = jnp.where(first, 1.0, 2.0).astype(jnp.float32)[:, :, None] / lon_count
    four_cos = f[0] * scaling
    four_sin = -f[1] * scaling
    grid = jnp.transpose(squared, (2, 0, 1)).reshape(signals, lon_count)
    return grid, four_cos, four_sin


def shards(coeffs, legendre, orders, lat_map, weights):
    slot_cap = coeffs.shape[0]
    epoch_count = coeffs.shape[1]
    deg_count = legendre.shape[1]
    half_lats = legendre.shape[2]
    lon_count = 2 * deg_count
    lat_rows = lat_map.shape[0]
    devices = lax.axis_size(("gx", "gy"))
    rows_each = lat_rows // devices

    synth = synthesize(coeffs, legendre, orders).reshape(slot_cap, 2, epoch_count * 2, half_lats)
    full_lats = jnp.concatenate([synth[:, 0], synth[:, 1, :, ::-1]], axis=-1)

    onehot = one_hot_rows(lat_map, lat_rows)
    permuted = jnp.einsum(
        "sxk,kr->sxr", full_lats, onehot, preferred_element_type=jnp.float32
    ).astype(jnp.bfloat16)
    sends = permuted.reshape(slot_cap, epoch_count * 2, devices, rows_each)
    sends = jnp.transpose(sends, (2, 0, 1, 3)).reshape(devices, slot_cap, epoch_count * 2 * rows_each)
    inner = inner_length(lon_count)
    outer = lon_count // inner
    blocks = deg_count // outer
    block_of = jnp.where(orders >= 0, orders // outer, -1)
    order_code = jnp.stack([block_of, orders % outer], axis=-1).astype(jnp.bfloat16)
    order_code = jnp.broadcast_to(order_code[None], (devices, slot_cap, 2))
    payload = jnp.concatenate([sends, order_code], axis=-1).reshape(devices, -1)
    width = payload.shape[1]
    padded = -(-width // 256) * 256
    payload = jnp.pad(payload, ((0, 0), (0, padded - width))).reshape(devices, padded // 128, 128)
    got = lax.all_to_all(payload, ("gx", "gy"), 0, 0, tiled=True)
    got = got.reshape(devices, padded)[:, :width].reshape(devices * slot_cap, -1)
    data = got[:, :-2]
    by_d = (got[:, -1:] == jnp.arange(outer, dtype=jnp.bfloat16)[None, :]).astype(jnp.bfloat16)
    in_c = got[:, -2:-1] == jnp.arange(blocks, dtype=jnp.bfloat16)[None, :]
    spread = jnp.where(in_c[:, :, None], data[:, None, :], jnp.zeros((), jnp.bfloat16))
    dense = jnp.einsum("sd,scr->dcr", by_d, spread, preferred_element_type=jnp.float32)
    dense = dense.reshape(outer, blocks, epoch_count, 2, rows_each)
    x_parts = jnp.stack([dense[:, :, :, 0, :], -dense[:, :, :, 1, :]])
    x_parts = jnp.transpose(x_parts, (0, 1, 2, 4, 3)).reshape(2, outer, blocks, rows_each * epoch_count)
    grid, four_cos, four_sin = transform_blocks(x_parts, lon_count)
    grid_rows = grid.reshape(rows_each, epoch_count, lon_count)

    split = (blocks, outer, rows_each, epoch_count)
    fourier = jnp.stack([four_cos.reshape(split), four_sin.reshape(split)], axis=4)
    fourier = jnp.transpose(fourier, (0, 1, 3, 4, 2))
    fourier = fourier.astype(jnp.bfloat16).reshape(blocks, outer, -1)
    picked = jnp.einsum("sd,cdr->scr", by_d, fourier, preferred_element_type=jnp.float32)
    by_slot = jnp.sum(jnp.where(in_c[:, :, None], picked, jnp.float32(0.0)), axis=1)
    back = by_slot.astype(jnp.bfloat16).reshape(devices, -1)
    width = back.shape[1]
    padded = -(-width // 256) * 256
    back = jnp.pad(back, ((0, 0), (0, padded - width))).reshape(devices, padded // 128, 128)
    back = lax.all_to_all(back, ("gx", "gy"), 0, 0, tiled=True)
    back = back.reshape(devices, padded)[:, :width].reshape(devices, slot_cap, epoch_count, 2, rows_each)
    returned = jnp.transpose(back, (1, 2, 3, 0, 4)).reshape(slot_cap, epoch_count * 2, lat_rows)
    natural = jnp.einsum(
        "sxr,kr->sxk", returned, onehot, preferred_element_type=jnp.float32
    )
    northern = natural[..., :half_lats]
    southern = natural[..., half_lats:][..., ::-1]
    sym_part = ((northern + southern) * weights).astype(jnp.bfloat16)
    anti_part = ((northern - southern) * weights).astype(jnp.bfloat16)
    both = jnp.concatenate([sym_part, anti_part], axis=1)
    spectra = analyze(both, legendre, orders, epoch_count, 2)
    return (grid_rows, spectra)


def solution(mesh):
    placed = (
        P(("gx", "gy"), None, None, None),
        P(("gx", "gy"), None, None),
        P(("gx", "gy")),
        P(),
        P(),
    )
    return jax.shard_map(
        shards,
        mesh=mesh,
        in_specs=placed,
        out_specs=(P(("gx", "gy"), None, None), P(("gx", "gy"), None, None, None)),
        check_vma=False,
    )
```

```python
import math

import jax
import jax.numpy as jnp
from jax import lax
from jax.experimental import pallas as pl
from jax.experimental.pallas import tpu as pltpu
from jax.sharding import PartitionSpec as P


SLOTS_PER_STEP = 12


def _masks(order, deg_count):
    degrees = lax.broadcasted_iota(jnp.int32, (1, deg_count), 1)
    usable = (degrees >= order) & (order >= 0)
    even = ((degrees + order) & 1) == 0
    return usable, even


def _synth_kernel(orders_ref, coef_ref, leg_ref, out_ref):
    step = pl.program_id(0)
    block, epochs, _, deg_count = coef_ref.shape
    zero = jnp.zeros((), coef_ref.dtype)
    for i in range(block):
        order = orders_ref[step * block + i]
        usable, even = _masks(order, deg_count)
        rows = jnp.concatenate([coef_ref[i, e] for e in range(epochs)], axis=0)
        masked = jnp.where(usable, rows, zero)
        signed = jnp.where(even, masked, -masked)
        lhs = jnp.concatenate([masked, signed], axis=0)
        out_ref[i] = jnp.dot(lhs, leg_ref[i], preferred_element_type=jnp.float32).astype(out_ref.dtype)


def synthesize(coeffs, legendre, orders):
    slot_cap, epochs, parts, deg_count = coeffs.shape
    half_lats = legendre.shape[2]
    block = SLOTS_PER_STEP
    rows = 2 * epochs * parts
    grid_spec = pltpu.PrefetchScalarGridSpec(
        num_scalar_prefetch=1,
        grid=(slot_cap // block,),
        in_specs=[
            pl.BlockSpec((block, epochs, parts, deg_count), lambda g, o: (g, 0, 0, 0)),
            pl.BlockSpec((block, deg_count, half_lats), lambda g, o: (g, 0, 0)),
        ],
        out_specs=pl.BlockSpec((block, rows, half_lats), lambda g, o: (g, 0, 0)),
    )
    return pl.pallas_call(
        _synth_kernel,
        grid_spec=grid_spec,
        out_shape=jax.ShapeDtypeStruct((slot_cap, rows, half_lats), jnp.bfloat16),
        compiler_params=pltpu.CompilerParams(dimension_semantics=("arbitrary",)),
        cost_estimate=pl.CostEstimate(
            flops=2 * slot_cap * rows * deg_count * half_lats,
            bytes_accessed=legendre.size * 2 + coeffs.size * 2 + slot_cap * rows * half_lats * 2,
            transcendentals=0,
        ),
    )(orders, coeffs, legendre)


def _analysis_kernel(orders_ref, both_ref, leg_ref, out_ref):
    step = pl.program_id(0)
    block, epochs, parts, deg_count = out_ref.shape
    half = epochs * parts
    for i in range(block):
        order = orders_ref[step * block + i]
        usable, even = _masks(order, deg_count)
        res = lax.dot_general(
            both_ref[i], leg_ref[i], (((1,), (1,)), ((), ())), preferred_element_type=jnp.float32
        )
        chosen = jnp.where(even, res[:half], res[half:])
        chosen = jnp.where(usable, chosen, jnp.float32(0.0)).astype(out_ref.dtype)
        for e in range(epochs):
            out_ref[i, e] = chosen[e * parts:(e + 1) * parts]


def analyze(both, legendre, orders, epochs, parts):
    slot_cap, rows, half_lats = both.shape
    deg_count = legendre.shape[1]
    block = SLOTS_PER_STEP
    grid_spec = pltpu.PrefetchScalarGridSpec(
        num_scalar_prefetch=1,
        grid=(slot_cap // block,),
        in_specs=[
            pl.BlockSpec((block, rows, half_lats), lambda g, o: (g, 0, 0)),
            pl.BlockSpec((block, deg_count, half_lats), lambda g, o: (g, 0, 0)),
        ],
        out_specs=pl.BlockSpec((block, epochs, parts, deg_count), lambda g, o: (g, 0, 0, 0)),
    )
    return pl.pallas_call(
        _analysis_kernel,
        grid_spec=grid_spec,
        out_shape=jax.ShapeDtypeStruct((slot_cap, epochs, parts, deg_count), jnp.bfloat16),
        compiler_params=pltpu.CompilerParams(dimension_semantics=("arbitrary",)),
        cost_estimate=pl.CostEstimate(
            flops=2 * slot_cap * rows * deg_count * half_lats,
            bytes_accessed=legendre.size * 2 + both.size * 2 + slot_cap * epochs * parts * deg_count * 2,
            transcendentals=0,
        ),
    )(orders, both, legendre)


def inner_length(lon_count):
    best = 1
    for factor in range(1, math.isqrt(lon_count) + 1):
        if lon_count % factor == 0:
            best = factor
    return best


def one_hot_rows(lat_map, lat_rows):
    return (lat_map[None, :] == jnp.arange(lat_rows, dtype=jnp.int32)[:, None]).astype(jnp.bfloat16)


def angle(numer, denom):
    return jnp.float32(2.0 * math.pi) * (numer % denom).astype(jnp.float32) / jnp.float32(denom)


def transform_blocks(x_parts, lon_count):
    highest = lax.Precision.HIGH
    _, outer, blocks, signals = x_parts.shape
    inner = lon_count // outer
    a_idx = jnp.arange(outer, dtype=jnp.int32)
    b_idx = jnp.arange(inner, dtype=jnp.int32)
    c_idx = jnp.arange(blocks, dtype=jnp.int32)
    w1 = angle(b_idx[:, None] * c_idx[None, :], inner)
    w1c, w1s = jnp.cos(w1), jnp.sin(w1)
    tw = angle(b_idx[:, None] * a_idx[None, :], lon_count)
    twc, tws = jnp.cos(tw)[:, :, None], jnp.sin(tw)[:, :, None]
    w2 = angle(a_idx[:, None] * a_idx[None, :], outer)
    w2c, w2s = jnp.cos(w2), jnp.sin(w2)

    def mm(spec, left, right):
        return jnp.einsum(spec, left, right, precision=highest)

    rot1 = jnp.stack([jnp.stack([w1c, -w1s]), jnp.stack([w1s, w1c])])
    y = mm("kjbc,jdcq->kbdq", rot1, x_parts)
    t_re = y[0] * twc - y[1] * tws
    t_im = y[0] * tws + y[1] * twc
    field = mm("jad,jbdq->abq", jnp.stack([w2c, -w2s]), jnp.stack([t_re, t_im]))
    squared = (field * field).astype(jnp.bfloat16)
    sq = squared.astype(jnp.float32)
    z = mm("kda,abq->kbdq", jnp.stack([w2c, -w2s]), sq)
    u_re = z[0] * twc + z[1] * tws
    u_im = z[1] * twc - z[0] * tws
    rot2 = jnp.stack([jnp.stack([w1c, w1s]), jnp.stack([-w1s, w1c])])
    f = mm("kjbc,jbdq->kcdq", rot2, jnp.stack([u_re, u_im]))
    first = (c_idx[:, None] == 0) & (a_idx[None, :] == 0)
    scaling = jnp.where(first, 1.0, 2.0).astype(jnp.float32)[:, :, None] / lon_count
    four_cos = f[0] * scaling
    four_sin = -f[1] * scaling
    grid = jnp.transpose(squared, (2, 0, 1)).reshape(signals, lon_count)
    return grid, four_cos, four_sin


def shards(coeffs, legendre, orders, lat_map, weights):
    slot_cap = coeffs.shape[0]
    epoch_count = coeffs.shape[1]
    deg_count = legendre.shape[1]
    half_lats = legendre.shape[2]
    lon_count = 2 * deg_count
    lat_rows = lat_map.shape[0]
    devices = lax.axis_size(("gx", "gy"))
    rows_each = lat_rows // devices

    synth = synthesize(coeffs, legendre, orders).reshape(slot_cap, 2, epoch_count * 2, half_lats)
    full_lats = jnp.concatenate([synth[:, 0], synth[:, 1, :, ::-1]], axis=-1)

    onehot = one_hot_rows(lat_map, lat_rows)
    permuted = jnp.einsum(
        "sxk,kr->sxr", full_lats, onehot, preferred_element_type=jnp.float32
    ).astype(jnp.bfloat16)
    sends = permuted.reshape(slot_cap, epoch_count * 2, devices, rows_each)
    sends = jnp.transpose(sends, (2, 0, 1, 3)).reshape(devices, slot_cap, epoch_count * 2 * rows_each)
    inner = inner_length(lon_count)
    outer = lon_count // inner
    blocks = deg_count // outer
    block_of = jnp.where(orders >= 0, orders // outer, -1)
    order_code = jnp.stack([block_of, orders % outer], axis=-1).astype(jnp.bfloat16)
    order_code = jnp.broadcast_to(order_code[None], (devices, slot_cap, 2))
    payload = jnp.concatenate([order_code, sends], axis=-1).reshape(devices, -1)
    width = payload.shape[1]
    padded = -(-width // 256) * 256
    payload = jnp.pad(payload, ((0, 0), (0, padded - width))).reshape(devices, padded // 128, 128)
    got = lax.all_to_all(payload, ("gx", "gy"), 0, 0, tiled=True)
    got = got.reshape(devices, padded)[:, :width].reshape(devices * slot_cap, -1)
    data = got[:, 2:]
    by_d = (got[:, 1:2] == jnp.arange(outer, dtype=jnp.bfloat16)[None, :]).astype(jnp.bfloat16)
    in_c = got[:, 0:1] == jnp.arange(blocks, dtype=jnp.bfloat16)[None, :]
    spread = jnp.where(in_c[:, :, None], data[:, None, :], jnp.zeros((), jnp.bfloat16))
    dense = jnp.einsum("sd,scr->dcr", by_d, spread, preferred_element_type=jnp.float32)
    dense = dense.reshape(outer, blocks, epoch_count, 2, rows_each)
    x_parts = jnp.stack([dense[:, :, :, 0, :], -dense[:, :, :, 1, :]])
    x_parts = jnp.transpose(x_parts, (0, 1, 2, 4, 3)).reshape(2, outer, blocks, rows_each * epoch_count)
    grid, four_cos, four_sin = transform_blocks(x_parts, lon_count)
    grid_rows = grid.reshape(rows_each, epoch_count, lon_count)

    split = (blocks, outer, rows_each, epoch_count)
    fourier = jnp.stack([four_cos.reshape(split), four_sin.reshape(split)], axis=4)
    fourier = jnp.transpose(fourier, (0, 1, 3, 4, 2))
    fourier = fourier.astype(jnp.bfloat16).reshape(blocks, outer, -1)
    picked = jnp.einsum("sd,cdr->scr", by_d, fourier, preferred_element_type=jnp.float32)
    by_slot = jnp.sum(jnp.where(in_c[:, :, None], picked, jnp.float32(0.0)), axis=1)
    back = by_slot.astype(jnp.bfloat16).reshape(devices, -1)
    width = back.shape[1]
    padded = -(-width // 256) * 256
    back = jnp.pad(back, ((0, 0), (0, padded - width))).reshape(devices, padded // 128, 128)
    back = lax.all_to_all(back, ("gx", "gy"), 0, 0, tiled=True)
    back = back.reshape(devices, padded)[:, :width].reshape(devices, slot_cap, epoch_count, 2, rows_each)
    returned = jnp.transpose(back, (1, 2, 3, 0, 4)).reshape(slot_cap, epoch_count * 2, lat_rows)
    natural = jnp.einsum(
        "sxr,kr->sxk", returned, onehot, preferred_element_type=jnp.float32
    )
    northern = natural[..., :half_lats]
    southern = natural[..., half_lats:][..., ::-1]
    sym_part = ((northern + southern) * weights).astype(jnp.bfloat16)
    anti_part = ((northern - southern) * weights).astype(jnp.bfloat16)
    both = jnp.concatenate([sym_part, anti_part], axis=1)
    spectra = analyze(both, legendre, orders, epoch_count, 2)
    return (grid_rows, spectra)


def solution(mesh):
    placed = (
        P(("gx", "gy"), None, None, None),
        P(("gx", "gy"), None, None),
        P(("gx", "gy")),
        P(),
        P(),
    )
    return jax.shard_map(
        shards,
        mesh=mesh,
        in_specs=placed,
        out_specs=(P(("gx", "gy"), None, None), P(("gx", "gy"), None, None, None)),
        check_vma=False,
    )
```

```python
import math

import jax
import jax.numpy as jnp
from jax import lax
from jax.experimental import pallas as pl
from jax.experimental.pallas import tpu as pltpu
from jax.sharding import PartitionSpec as P


SLOTS_PER_STEP = 12


def _masks(order, deg_count):
    degrees = lax.broadcasted_iota(jnp.int32, (1, deg_count), 1)
    usable = (degrees >= order) & (order >= 0)
    even = ((degrees + order) & 1) == 0
    return usable, even


def _synth_kernel(orders_ref, coef_ref, leg_ref, out_ref):
    step = pl.program_id(0)
    block, epochs, _, deg_count = coef_ref.shape
    zero = jnp.zeros((), coef_ref.dtype)
    for i in range(block):
        order = orders_ref[step * block + i]
        usable, even = _masks(order, deg_count)
        rows = jnp.concatenate([coef_ref[i, e] for e in range(epochs)], axis=0)
        masked = jnp.where(usable, rows, zero)
        signed = jnp.where(even, masked, -masked)
        lhs = jnp.concatenate([masked, signed], axis=0)
        out_ref[i] = jnp.dot(lhs, leg_ref[i], preferred_element_type=jnp.float32).astype(out_ref.dtype)


def synthesize(coeffs, legendre, orders):
    slot_cap, epochs, parts, deg_count = coeffs.shape
    half_lats = legendre.shape[2]
    block = SLOTS_PER_STEP
    rows = 2 * epochs * parts
    grid_spec = pltpu.PrefetchScalarGridSpec(
        num_scalar_prefetch=1,
        grid=(slot_cap // block,),
        in_specs=[
            pl.BlockSpec((block, epochs, parts, deg_count), lambda g, o: (g, 0, 0, 0)),
            pl.BlockSpec((block, deg_count, half_lats), lambda g, o: (g, 0, 0)),
        ],
        out_specs=pl.BlockSpec((block, rows, half_lats), lambda g, o: (g, 0, 0)),
    )
    return pl.pallas_call(
        _synth_kernel,
        grid_spec=grid_spec,
        out_shape=jax.ShapeDtypeStruct((slot_cap, rows, half_lats), jnp.bfloat16),
        compiler_params=pltpu.CompilerParams(dimension_semantics=("arbitrary",)),
        cost_estimate=pl.CostEstimate(
            flops=2 * slot_cap * rows * deg_count * half_lats,
            bytes_accessed=legendre.size * 2 + coeffs.size * 2 + slot_cap * rows * half_lats * 2,
            transcendentals=0,
        ),
    )(orders, coeffs, legendre)


def _analysis_kernel(orders_ref, both_ref, leg_ref, out_ref):
    step = pl.program_id(0)
    block, epochs, parts, deg_count = out_ref.shape
    half = epochs * parts
    for i in range(block):
        order = orders_ref[step * block + i]
        usable, even = _masks(order, deg_count)
        res = lax.dot_general(
            both_ref[i], leg_ref[i], (((1,), (1,)), ((), ())), preferred_element_type=jnp.float32
        )
        chosen = jnp.where(even, res[:half], res[half:])
        chosen = jnp.where(usable, chosen, jnp.float32(0.0)).astype(out_ref.dtype)
        for e in range(epochs):
            out_ref[i, e] = chosen[e * parts:(e + 1) * parts]


def analyze(both, legendre, orders, epochs, parts):
    slot_cap, rows, half_lats = both.shape
    deg_count = legendre.shape[1]
    block = SLOTS_PER_STEP
    grid_spec = pltpu.PrefetchScalarGridSpec(
        num_scalar_prefetch=1,
        grid=(slot_cap // block,),
        in_specs=[
            pl.BlockSpec((block, rows, half_lats), lambda g, o: (g, 0, 0)),
            pl.BlockSpec((block, deg_count, half_lats), lambda g, o: (g, 0, 0)),
        ],
        out_specs=pl.BlockSpec((block, epochs, parts, deg_count), lambda g, o: (g, 0, 0, 0)),
    )
    return pl.pallas_call(
        _analysis_kernel,
        grid_spec=grid_spec,
        out_shape=jax.ShapeDtypeStruct((slot_cap, epochs, parts, deg_count), jnp.bfloat16),
        compiler_params=pltpu.CompilerParams(dimension_semantics=("arbitrary",)),
        cost_estimate=pl.CostEstimate(
            flops=2 * slot_cap * rows * deg_count * half_lats,
            bytes_accessed=legendre.size * 2 + both.size * 2 + slot_cap * epochs * parts * deg_count * 2,
            transcendentals=0,
        ),
    )(orders, both, legendre)


def inner_length(lon_count):
    best = 1
    for factor in range(1, math.isqrt(lon_count) + 1):
        if lon_count % factor == 0:
            best = factor
    return best


def one_hot_rows(lat_map, lat_rows):
    half = lat_rows // 2
    slot = jnp.arange(lat_rows, dtype=jnp.int32)
    latitude = jnp.where(slot < half, slot, lat_rows + half - 1 - slot)
    return (lat_map[None, :] == latitude[:, None]).astype(jnp.bfloat16)


def angle(numer, denom):
    return jnp.float32(2.0 * math.pi) * (numer % denom).astype(jnp.float32) / jnp.float32(denom)


def transform_blocks(x_parts, lon_count):
    highest = lax.Precision.HIGH
    _, outer, blocks, signals = x_parts.shape
    inner = lon_count // outer
    a_idx = jnp.arange(outer, dtype=jnp.int32)
    b_idx = jnp.arange(inner, dtype=jnp.int32)
    c_idx = jnp.arange(blocks, dtype=jnp.int32)
    w1 = angle(b_idx[:, None] * c_idx[None, :], inner)
    w1c, w1s = jnp.cos(w1), jnp.sin(w1)
    tw = angle(b_idx[:, None] * a_idx[None, :], lon_count)
    twc, tws = jnp.cos(tw)[:, :, None], jnp.sin(tw)[:, :, None]
    w2 = angle(a_idx[:, None] * a_idx[None, :], outer)
    w2c, w2s = jnp.cos(w2), jnp.sin(w2)

    def mm(spec, left, right):
        return jnp.einsum(spec, left, right, precision=highest)

    rot1 = jnp.stack([jnp.stack([w1c, -w1s]), jnp.stack([w1s, w1c])])
    y = mm("kjbc,jdcq->kbdq", rot1, x_parts)
    t_re = y[0] * twc - y[1] * tws
    t_im = y[0] * tws + y[1] * twc
    field = mm("jad,jbdq->abq", jnp.stack([w2c, -w2s]), jnp.stack([t_re, t_im]))
    squared = (field * field).astype(jnp.bfloat16)
    sq = squared.astype(jnp.float32)
    z = mm("kda,abq->kbdq", jnp.stack([w2c, -w2s]), sq)
    u_re = z[0] * twc + z[1] * tws
    u_im = z[1] * twc - z[0] * tws
    rot2 = jnp.stack([jnp.stack([w1c, w1s]), jnp.stack([-w1s, w1c])])
    f = mm("kjbc,jbdq->kcdq", rot2, jnp.stack([u_re, u_im]))
    first = (c_idx[:, None] == 0) & (a_idx[None, :] == 0)
    scaling = jnp.where(first, 1.0, 2.0).astype(jnp.float32)[:, :, None] / lon_count
    four_cos = f[0] * scaling
    four_sin = -f[1] * scaling
    grid = jnp.transpose(squared, (2, 0, 1)).reshape(signals, lon_count)
    return grid, four_cos, four_sin


def shards(coeffs, legendre, orders, lat_map, weights):
    slot_cap = coeffs.shape[0]
    epoch_count = coeffs.shape[1]
    deg_count = legendre.shape[1]
    half_lats = legendre.shape[2]
    lon_count = 2 * deg_count
    lat_rows = lat_map.shape[0]
    devices = lax.axis_size(("gx", "gy"))
    rows_each = lat_rows // devices

    synth = synthesize(coeffs, legendre, orders).reshape(slot_cap, 2, epoch_count * 2, half_lats)
    full_lats = jnp.concatenate([synth[:, 0], synth[:, 1]], axis=-1)

    onehot = one_hot_rows(lat_map, lat_rows)
    permuted = jnp.einsum(
        "sxk,kr->sxr", full_lats, onehot, preferred_element_type=jnp.float32
    ).astype(jnp.bfloat16)
    sends = permuted.reshape(slot_cap, epoch_count * 2, devices, rows_each)
    sends = jnp.transpose(sends, (2, 0, 1, 3)).reshape(devices, slot_cap, epoch_count * 2 * rows_each)
    inner = inner_length(lon_count)
    outer = lon_count // inner
    blocks = deg_count // outer
    block_of = jnp.where(orders >= 0, orders // outer, -1)
    order_code = jnp.stack([block_of, orders % outer], axis=-1).astype(jnp.bfloat16)
    order_code = jnp.broadcast_to(order_code[None], (devices, slot_cap, 2))
    payload = jnp.concatenate([sends, order_code], axis=-1).reshape(devices, -1)
    width = payload.shape[1]
    padded = -(-width // 256) * 256
    payload = jnp.pad(payload, ((0, 0), (0, padded - width))).reshape(devices, padded // 128, 128)
    got = lax.all_to_all(payload, ("gx", "gy"), 0, 0, tiled=True)
    got = got.reshape(devices, padded)[:, :width].reshape(devices * slot_cap, -1)
    data = got[:, :-2]
    by_d = (got[:, -1:] == jnp.arange(outer, dtype=jnp.bfloat16)[None, :]).astype(jnp.bfloat16)
    in_c = got[:, -2:-1] == jnp.arange(blocks, dtype=jnp.bfloat16)[None, :]
    spread = jnp.where(in_c[:, :, None], data[:, None, :], jnp.zeros((), jnp.bfloat16))
    dense = jnp.einsum("sd,scr->dcr", by_d, spread, preferred_element_type=jnp.float32)
    dense = dense.reshape(outer, blocks, epoch_count, 2, rows_each)
    x_parts = jnp.stack([dense[:, :, :, 0, :], -dense[:, :, :, 1, :]])
    x_parts = jnp.transpose(x_parts, (0, 1, 2, 4, 3)).reshape(2, outer, blocks, rows_each * epoch_count)
    grid, four_cos, four_sin = transform_blocks(x_parts, lon_count)
    grid_rows = grid.reshape(rows_each, epoch_count, lon_count)

    split = (blocks, outer, rows_each, epoch_count)
    fourier = jnp.stack([four_cos.reshape(split), four_sin.reshape(split)], axis=4)
    fourier = jnp.transpose(fourier, (0, 1, 3, 4, 2))
    fourier = fourier.astype(jnp.bfloat16).reshape(blocks, outer, -1)
    picked = jnp.einsum("sd,cdr->scr", by_d, fourier, preferred_element_type=jnp.float32)
    by_slot = jnp.sum(jnp.where(in_c[:, :, None], picked, jnp.float32(0.0)), axis=1)
    back = by_slot.astype(jnp.bfloat16).reshape(devices, -1)
    width = back.shape[1]
    padded = -(-width // 256) * 256
    back = jnp.pad(back, ((0, 0), (0, padded - width))).reshape(devices, padded // 128, 128)
    back = lax.all_to_all(back, ("gx", "gy"), 0, 0, tiled=True)
    back = back.reshape(devices, padded)[:, :width].reshape(devices, slot_cap, epoch_count, 2, rows_each)
    returned = jnp.transpose(back, (1, 2, 3, 0, 4)).reshape(slot_cap, epoch_count * 2, lat_rows)
    natural = jnp.einsum(
        "sxr,kr->sxk", returned, onehot, preferred_element_type=jnp.float32
    )
    northern = natural[..., :half_lats]
    southern = natural[..., half_lats:]
    sym_part = ((northern + southern) * weights).astype(jnp.bfloat16)
    anti_part = ((northern - southern) * weights).astype(jnp.bfloat16)
    both = jnp.concatenate([sym_part, anti_part], axis=1)
    spectra = analyze(both, legendre, orders, epoch_count, 2)
    return (grid_rows, spectra)


def solution(mesh):
    placed = (
        P(("gx", "gy"), None, None, None),
        P(("gx", "gy"), None, None),
        P(("gx", "gy")),
        P(),
        P(),
    )
    return jax.shard_map(
        shards,
        mesh=mesh,
        in_specs=placed,
        out_specs=(P(("gx", "gy"), None, None), P(("gx", "gy"), None, None, None)),
        check_vma=False,
    )
```

```python
import math

import jax
import jax.numpy as jnp
from jax import lax
from jax.experimental import pallas as pl
from jax.experimental.pallas import tpu as pltpu
from jax.sharding import PartitionSpec as P


SLOTS_PER_STEP = 12


def _masks(order, deg_count):
    degrees = lax.broadcasted_iota(jnp.int32, (1, deg_count), 1)
    usable = (degrees >= order) & (order >= 0)
    even = ((degrees + order) & 1) == 0
    return usable, even


def _synth_kernel(orders_ref, coef_ref, leg_ref, out_ref):
    step = pl.program_id(0)
    block, epochs, _, deg_count = coef_ref.shape
    zero = jnp.zeros((), coef_ref.dtype)
    for i in range(block):
        order = orders_ref[step * block + i]
        usable, even = _masks(order, deg_count)
        rows = jnp.concatenate([coef_ref[i, e] for e in range(epochs)], axis=0)
        masked = jnp.where(usable, rows, zero)
        signed = jnp.where(even, masked, -masked)
        lhs = jnp.concatenate([masked, signed], axis=0)
        out_ref[i] = jnp.dot(lhs, leg_ref[i], preferred_element_type=jnp.float32).astype(out_ref.dtype)


def synthesize(coeffs, legendre, orders):
    slot_cap, epochs, parts, deg_count = coeffs.shape
    half_lats = legendre.shape[2]
    block = SLOTS_PER_STEP
    rows = 2 * epochs * parts
    grid_spec = pltpu.PrefetchScalarGridSpec(
        num_scalar_prefetch=1,
        grid=(slot_cap // block,),
        in_specs=[
            pl.BlockSpec((block, epochs, parts, deg_count), lambda g, o: (g, 0, 0, 0)),
            pl.BlockSpec((block, deg_count, half_lats), lambda g, o: (g, 0, 0)),
        ],
        out_specs=pl.BlockSpec((block, rows, half_lats), lambda g, o: (g, 0, 0)),
    )
    return pl.pallas_call(
        _synth_kernel,
        grid_spec=grid_spec,
        out_shape=jax.ShapeDtypeStruct((slot_cap, rows, half_lats), jnp.bfloat16),
        compiler_params=pltpu.CompilerParams(dimension_semantics=("arbitrary",)),
        cost_estimate=pl.CostEstimate(
            flops=2 * slot_cap * rows * deg_count * half_lats,
            bytes_accessed=legendre.size * 2 + coeffs.size * 2 + slot_cap * rows * half_lats * 2,
            transcendentals=0,
        ),
    )(orders, coeffs, legendre)


def _analysis_kernel(orders_ref, sym_ref, anti_ref, leg_ref, out_ref):
    step = pl.program_id(0)
    block, epochs, parts, deg_count = out_ref.shape
    half = epochs * parts
    for i in range(block):
        order = orders_ref[step * block + i]
        usable, even = _masks(order, deg_count)
        res = lax.dot_general(
            jnp.concatenate([sym_ref[i], anti_ref[i]], axis=0), leg_ref[i], (((1,), (1,)), ((), ())),
            preferred_element_type=jnp.float32,
        )
        chosen = jnp.where(even, res[:half], res[half:])
        chosen = jnp.where(usable, chosen, jnp.float32(0.0)).astype(out_ref.dtype)
        for e in range(epochs):
            out_ref[i, e] = chosen[e * parts:(e + 1) * parts]


def analyze(sym, anti, legendre, orders, epochs, parts):
    slot_cap, half, half_lats = sym.shape
    rows = 2 * half
    deg_count = legendre.shape[1]
    block = SLOTS_PER_STEP
    grid_spec = pltpu.PrefetchScalarGridSpec(
        num_scalar_prefetch=1,
        grid=(slot_cap // block,),
        in_specs=[
            pl.BlockSpec((block, half, half_lats), lambda g, o: (g, 0, 0)),
            pl.BlockSpec((block, half, half_lats), lambda g, o: (g, 0, 0)),
            pl.BlockSpec((block, deg_count, half_lats), lambda g, o: (g, 0, 0)),
        ],
        out_specs=pl.BlockSpec((block, epochs, parts, deg_count), lambda g, o: (g, 0, 0, 0)),
    )
    return pl.pallas_call(
        _analysis_kernel,
        grid_spec=grid_spec,
        out_shape=jax.ShapeDtypeStruct((slot_cap, epochs, parts, deg_count), jnp.bfloat16),
        compiler_params=pltpu.CompilerParams(dimension_semantics=("arbitrary",)),
        cost_estimate=pl.CostEstimate(
            flops=2 * slot_cap * rows * deg_count * half_lats,
            bytes_accessed=legendre.size * 2 + 2 * sym.size * 2 + slot_cap * epochs * parts * deg_count * 2,
            transcendentals=0,
        ),
    )(orders, sym, anti, legendre)


def inner_length(lon_count):
    best = 1
    for factor in range(1, math.isqrt(lon_count) + 1):
        if lon_count % factor == 0:
            best = factor
    return best


def one_hot_rows(lat_map, lat_rows):
    return (lat_map[None, :] == jnp.arange(lat_rows, dtype=jnp.int32)[:, None]).astype(jnp.bfloat16)


def angle(numer, denom):
    return jnp.float32(2.0 * math.pi) * (numer % denom).astype(jnp.float32) / jnp.float32(denom)


def transform_blocks(x_parts, lon_count):
    highest = lax.Precision.HIGH
    _, outer, blocks, signals = x_parts.shape
    inner = lon_count // outer
    a_idx = jnp.arange(outer, dtype=jnp.int32)
    b_idx = jnp.arange(inner, dtype=jnp.int32)
    c_idx = jnp.arange(blocks, dtype=jnp.int32)
    w1 = angle(b_idx[:, None] * c_idx[None, :], inner)
    w1c, w1s = jnp.cos(w1), jnp.sin(w1)
    tw = angle(b_idx[:, None] * a_idx[None, :], lon_count)
    twc, tws = jnp.cos(tw)[:, :, None], jnp.sin(tw)[:, :, None]
    w2 = angle(a_idx[:, None] * a_idx[None, :], outer)
    w2c, w2s = jnp.cos(w2), jnp.sin(w2)

    def mm(spec, left, right):
        return jnp.einsum(spec, left, right, precision=highest)

    rot1 = jnp.stack([jnp.stack([w1c, -w1s]), jnp.stack([w1s, w1c])])
    y = mm("kjbc,jdcq->kbdq", rot1, x_parts)
    t_re = y[0] * twc - y[1] * tws
    t_im = y[0] * tws + y[1] * twc
    field = mm("jad,jbdq->abq", jnp.stack([w2c, -w2s]), jnp.stack([t_re, t_im]))
    squared = (field * field).astype(jnp.bfloat16)
    sq = squared.astype(jnp.float32)
    z = mm("kda,abq->kbdq", jnp.stack([w2c, -w2s]), sq)
    u_re = z[0] * twc + z[1] * tws
    u_im = z[1] * twc - z[0] * tws
    rot2 = jnp.stack([jnp.stack([w1c, w1s]), jnp.stack([-w1s, w1c])])
    f = mm("kjbc,jbdq->kcdq", rot2, jnp.stack([u_re, u_im]))
    first = (c_idx[:, None] == 0) & (a_idx[None, :] == 0)
    scaling = jnp.where(first, 1.0, 2.0).astype(jnp.float32)[:, :, None] / lon_count
    four_cos = f[0] * scaling
    four_sin = -f[1] * scaling
    grid = jnp.transpose(squared, (2, 0, 1)).reshape(signals, lon_count)
    return grid, four_cos, four_sin


def shards(coeffs, legendre, orders, lat_map, weights):
    slot_cap = coeffs.shape[0]
    epoch_count = coeffs.shape[1]
    deg_count = legendre.shape[1]
    half_lats = legendre.shape[2]
    lon_count = 2 * deg_count
    lat_rows = lat_map.shape[0]
    devices = lax.axis_size(("gx", "gy"))
    rows_each = lat_rows // devices

    synth = synthesize(coeffs, legendre, orders).reshape(slot_cap, 2, epoch_count * 2, half_lats)
    full_lats = jnp.concatenate([synth[:, 0], synth[:, 1, :, ::-1]], axis=-1)

    onehot = one_hot_rows(lat_map, lat_rows)
    permuted = jnp.einsum(
        "sxk,kr->sxr", full_lats, onehot, preferred_element_type=jnp.float32
    ).astype(jnp.bfloat16)
    sends = permuted.reshape(slot_cap, epoch_count * 2, devices, rows_each)
    sends = jnp.transpose(sends, (2, 0, 1, 3)).reshape(devices, slot_cap, epoch_count * 2 * rows_each)
    inner = inner_length(lon_count)
    outer = lon_count // inner
    blocks = deg_count // outer
    block_of = jnp.where(orders >= 0, orders // outer, -1)
    order_code = jnp.stack([block_of, orders % outer], axis=-1).astype(jnp.bfloat16)
    order_code = jnp.broadcast_to(order_code[None], (devices, slot_cap, 2))
    payload = jnp.concatenate([sends, order_code], axis=-1).reshape(devices, -1)
    width = payload.shape[1]
    padded = -(-width // 256) * 256
    payload = jnp.pad(payload, ((0, 0), (0, padded - width))).reshape(devices, padded // 128, 128)
    got = lax.all_to_all(payload, ("gx", "gy"), 0, 0, tiled=True)
    got = got.reshape(devices, padded)[:, :width].reshape(devices * slot_cap, -1)
    data = got[:, :-2]
    by_d = (got[:, -1:] == jnp.arange(outer, dtype=jnp.bfloat16)[None, :]).astype(jnp.bfloat16)
    in_c = got[:, -2:-1] == jnp.arange(blocks, dtype=jnp.bfloat16)[None, :]
    spread = jnp.where(in_c[:, :, None], data[:, None, :], jnp.zeros((), jnp.bfloat16))
    dense = jnp.einsum("sd,scr->dcr", by_d, spread, preferred_element_type=jnp.float32)
    dense = dense.reshape(outer, blocks, epoch_count, 2, rows_each)
    x_parts = jnp.stack([dense[:, :, :, 0, :], -dense[:, :, :, 1, :]])
    x_parts = jnp.transpose(x_parts, (0, 1, 2, 4, 3)).reshape(2, outer, blocks, rows_each * epoch_count)
    grid, four_cos, four_sin = transform_blocks(x_parts, lon_count)
    grid_rows = grid.reshape(rows_each, epoch_count, lon_count)

    split = (blocks, outer, rows_each, epoch_count)
    fourier = jnp.stack([four_cos.reshape(split), four_sin.reshape(split)], axis=4)
    fourier = jnp.transpose(fourier, (0, 1, 3, 4, 2))
    fourier = fourier.astype(jnp.bfloat16).reshape(blocks, outer, -1)
    picked = jnp.einsum("sd,cdr->scr", by_d, fourier, preferred_element_type=jnp.float32)
    by_slot = jnp.sum(jnp.where(in_c[:, :, None], picked, jnp.float32(0.0)), axis=1)
    back = by_slot.astype(jnp.bfloat16).reshape(devices, -1)
    width = back.shape[1]
    padded = -(-width // 256) * 256
    back = jnp.pad(back, ((0, 0), (0, padded - width))).reshape(devices, padded // 128, 128)
    back = lax.all_to_all(back, ("gx", "gy"), 0, 0, tiled=True)
    back = back.reshape(devices, padded)[:, :width].reshape(devices, slot_cap, epoch_count, 2, rows_each)
    returned = jnp.transpose(back, (1, 2, 3, 0, 4)).reshape(slot_cap, epoch_count * 2, lat_rows)
    natural = jnp.einsum(
        "sxr,kr->sxk", returned, onehot, preferred_element_type=jnp.float32
    )
    northern = natural[..., :half_lats]
    southern = natural[..., half_lats:][..., ::-1]
    sym_part = ((northern + southern) * weights).astype(jnp.bfloat16)
    anti_part = ((northern - southern) * weights).astype(jnp.bfloat16)
    spectra = analyze(sym_part, anti_part, legendre, orders, epoch_count, 2)
    return (grid_rows, spectra)


def solution(mesh):
    placed = (
        P(("gx", "gy"), None, None, None),
        P(("gx", "gy"), None, None),
        P(("gx", "gy")),
        P(),
        P(),
    )
    return jax.shard_map(
        shards,
        mesh=mesh,
        in_specs=placed,
        out_specs=(P(("gx", "gy"), None, None), P(("gx", "gy"), None, None, None)),
        check_vma=False,
    )
```

```python
import math

import jax
import jax.numpy as jnp
from jax import lax
from jax.experimental import pallas as pl
from jax.experimental.pallas import tpu as pltpu
from jax.sharding import PartitionSpec as P


SLOTS_PER_STEP = 12


def _masks(order, deg_count):
    degrees = lax.broadcasted_iota(jnp.int32, (1, deg_count), 1)
    usable = (degrees >= order) & (order >= 0)
    even = ((degrees + order) & 1) == 0
    return usable, even


def _synth_kernel(orders_ref, coef_ref, leg_ref, out_ref):
    step = pl.program_id(0)
    block, epochs, _, deg_count = coef_ref.shape
    zero = jnp.zeros((), coef_ref.dtype)
    for i in range(block):
        order = orders_ref[step * block + i]
        usable, even = _masks(order, deg_count)
        rows = jnp.concatenate([coef_ref[i, e] for e in range(epochs)], axis=0)
        masked = jnp.where(usable, rows, zero)
        signed = jnp.where(even, masked, -masked)
        lhs = jnp.concatenate([masked, signed], axis=0)
        out_ref[i] = jnp.dot(lhs, leg_ref[i], preferred_element_type=jnp.float32).astype(out_ref.dtype)


def synthesize(coeffs, legendre, orders):
    slot_cap, epochs, parts, deg_count = coeffs.shape
    half_lats = legendre.shape[2]
    block = SLOTS_PER_STEP
    rows = 2 * epochs * parts
    grid_spec = pltpu.PrefetchScalarGridSpec(
        num_scalar_prefetch=1,
        grid=(slot_cap // block,),
        in_specs=[
            pl.BlockSpec((block, epochs, parts, deg_count), lambda g, o: (g, 0, 0, 0)),
            pl.BlockSpec((block, deg_count, half_lats), lambda g, o: (g, 0, 0)),
        ],
        out_specs=pl.BlockSpec((block, rows, half_lats), lambda g, o: (g, 0, 0)),
    )
    return pl.pallas_call(
        _synth_kernel,
        grid_spec=grid_spec,
        out_shape=jax.ShapeDtypeStruct((slot_cap, rows, half_lats), jnp.bfloat16),
        compiler_params=pltpu.CompilerParams(dimension_semantics=("arbitrary",)),
        cost_estimate=pl.CostEstimate(
            flops=2 * slot_cap * rows * deg_count * half_lats,
            bytes_accessed=legendre.size * 2 + coeffs.size * 2 + slot_cap * rows * half_lats * 2,
            transcendentals=0,
        ),
    )(orders, coeffs, legendre)


def _analysis_kernel(orders_ref, sym_ref, anti_ref, leg_ref, out_ref):
    step = pl.program_id(0)
    block, epochs, parts, deg_count = out_ref.shape
    half = epochs * parts
    for i in range(block):
        order = orders_ref[step * block + i]
        usable, even = _masks(order, deg_count)
        res = lax.dot_general(
            jnp.concatenate([sym_ref[i], anti_ref[i]], axis=0), leg_ref[i], (((1,), (1,)), ((), ())),
            preferred_element_type=jnp.float32,
        )
        chosen = jnp.where(even, res[:half], res[half:])
        chosen = jnp.where(usable, chosen, jnp.float32(0.0)).astype(out_ref.dtype)
        for e in range(epochs):
            out_ref[i, e] = chosen[e * parts:(e + 1) * parts]


def analyze(sym, anti, legendre, orders, epochs, parts):
    slot_cap, half, half_lats = sym.shape
    rows = 2 * half
    deg_count = legendre.shape[1]
    block = SLOTS_PER_STEP
    grid_spec = pltpu.PrefetchScalarGridSpec(
        num_scalar_prefetch=1,
        grid=(slot_cap // block,),
        in_specs=[
            pl.BlockSpec((block, half, half_lats), lambda g, o: (g, 0, 0)),
            pl.BlockSpec((block, half, half_lats), lambda g, o: (g, 0, 0)),
            pl.BlockSpec((block, deg_count, half_lats), lambda g, o: (g, 0, 0)),
        ],
        out_specs=pl.BlockSpec((block, epochs, parts, deg_count), lambda g, o: (g, 0, 0, 0)),
    )
    return pl.pallas_call(
        _analysis_kernel,
        grid_spec=grid_spec,
        out_shape=jax.ShapeDtypeStruct((slot_cap, epochs, parts, deg_count), jnp.bfloat16),
        compiler_params=pltpu.CompilerParams(dimension_semantics=("arbitrary",)),
        cost_estimate=pl.CostEstimate(
            flops=2 * slot_cap * rows * deg_count * half_lats,
            bytes_accessed=legendre.size * 2 + 2 * sym.size * 2 + slot_cap * epochs * parts * deg_count * 2,
            transcendentals=0,
        ),
    )(orders, sym, anti, legendre)


def inner_length(lon_count):
    best = 1
    for factor in range(1, math.isqrt(lon_count) + 1):
        if lon_count % factor == 0:
            best = factor
    return best


def one_hot_rows(lat_map, lat_rows):
    half = lat_rows // 2
    slot = jnp.arange(lat_rows, dtype=jnp.int32)
    latitude = jnp.where(slot < half, slot, lat_rows + half - 1 - slot)
    return (lat_map[None, :] == latitude[:, None]).astype(jnp.bfloat16)


def angle(numer, denom):
    return jnp.float32(2.0 * math.pi) * (numer % denom).astype(jnp.float32) / jnp.float32(denom)


def transform_blocks(x_parts, lon_count):
    highest = lax.Precision.HIGH
    _, outer, blocks, signals = x_parts.shape
    inner = lon_count // outer
    a_idx = jnp.arange(outer, dtype=jnp.int32)
    b_idx = jnp.arange(inner, dtype=jnp.int32)
    c_idx = jnp.arange(blocks, dtype=jnp.int32)
    w1 = angle(b_idx[:, None] * c_idx[None, :], inner)
    w1c, w1s = jnp.cos(w1), jnp.sin(w1)
    tw = angle(b_idx[:, None] * a_idx[None, :], lon_count)
    twc, tws = jnp.cos(tw)[:, :, None], jnp.sin(tw)[:, :, None]
    w2 = angle(a_idx[:, None] * a_idx[None, :], outer)
    w2c, w2s = jnp.cos(w2), jnp.sin(w2)

    def mm(spec, left, right):
        return jnp.einsum(spec, left, right, precision=highest)

    rot1 = jnp.stack([jnp.stack([w1c, -w1s]), jnp.stack([w1s, w1c])])
    y = mm("kjbc,jdcq->kbdq", rot1, x_parts)
    t_re = y[0] * twc - y[1] * tws
    t_im = y[0] * tws + y[1] * twc
    field = mm("jad,jbdq->abq", jnp.stack([w2c, -w2s]), jnp.stack([t_re, t_im]))
    squared = (field * field).astype(jnp.bfloat16)
    sq = squared.astype(jnp.float32)
    z = mm("kda,abq->kbdq", jnp.stack([w2c, -w2s]), sq)
    u_re = z[0] * twc + z[1] * tws
    u_im = z[1] * twc - z[0] * tws
    rot2 = jnp.stack([jnp.stack([w1c, w1s]), jnp.stack([-w1s, w1c])])
    f = mm("kjbc,jbdq->kcdq", rot2, jnp.stack([u_re, u_im]))
    first = (c_idx[:, None] == 0) & (a_idx[None, :] == 0)
    scaling = jnp.where(first, 1.0, 2.0).astype(jnp.float32)[:, :, None] / lon_count
    four_cos = f[0] * scaling
    four_sin = -f[1] * scaling
    grid = jnp.transpose(squared, (2, 0, 1)).reshape(signals, lon_count)
    return grid, four_cos, four_sin


def shards(coeffs, legendre, orders, lat_map, weights):
    slot_cap = coeffs.shape[0]
    epoch_count = coeffs.shape[1]
    deg_count = legendre.shape[1]
    half_lats = legendre.shape[2]
    lon_count = 2 * deg_count
    lat_rows = lat_map.shape[0]
    devices = lax.axis_size(("gx", "gy"))
    rows_each = lat_rows // devices

    synth = synthesize(coeffs, legendre, orders).reshape(slot_cap, 2, epoch_count * 2, half_lats)
    full_lats = jnp.concatenate([synth[:, 0], synth[:, 1]], axis=-1)

    onehot = one_hot_rows(lat_map, lat_rows)
    permuted = jnp.einsum(
        "sxk,kr->sxr", full_lats, onehot, preferred_element_type=jnp.float32
    ).astype(jnp.bfloat16)
    sends = permuted.reshape(slot_cap, epoch_count * 2, devices, rows_each)
    sends = jnp.transpose(sends, (2, 0, 1, 3)).reshape(devices, slot_cap, epoch_count * 2 * rows_each)
    inner = inner_length(lon_count)
    outer = lon_count // inner
    blocks = deg_count // outer
    block_of = jnp.where(orders >= 0, orders // outer, -1)
    order_code = jnp.stack([block_of, orders % outer], axis=-1).astype(jnp.bfloat16)
    order_code = jnp.broadcast_to(order_code[None], (devices, slot_cap, 2))
    payload = jnp.concatenate([sends, order_code], axis=-1).reshape(devices, -1)
    width = payload.shape[1]
    padded = -(-width // 256) * 256
    payload = jnp.pad(payload, ((0, 0), (0, padded - width))).reshape(devices, padded // 128, 128)
    got = lax.all_to_all(payload, ("gx", "gy"), 0, 0, tiled=True)
    got = got.reshape(devices, padded)[:, :width].reshape(devices * slot_cap, -1)
    data = got[:, :-2]
    by_d = (got[:, -1:] == jnp.arange(outer, dtype=jnp.bfloat16)[None, :]).astype(jnp.bfloat16)
    in_c = got[:, -2:-1] == jnp.arange(blocks, dtype=jnp.bfloat16)[None, :]
    spread = jnp.where(in_c[:, :, None], data[:, None, :], jnp.zeros((), jnp.bfloat16))
    dense = jnp.einsum("sd,scr->dcr", by_d, spread, preferred_element_type=jnp.float32)
    dense = dense.reshape(outer, blocks, epoch_count, 2, rows_each)
    x_parts = jnp.stack([dense[:, :, :, 0, :], -dense[:, :, :, 1, :]])
    x_parts = jnp.transpose(x_parts, (0, 1, 2, 4, 3)).reshape(2, outer, blocks, rows_each * epoch_count)
    grid, four_cos, four_sin = transform_blocks(x_parts, lon_count)
    grid_rows = grid.reshape(rows_each, epoch_count, lon_count)

    split = (blocks, outer, rows_each, epoch_count)
    fourier = jnp.stack([four_cos.reshape(split), four_sin.reshape(split)], axis=4)
    fourier = jnp.transpose(fourier, (0, 1, 3, 4, 2))
    fourier = fourier.astype(jnp.bfloat16).reshape(blocks, outer, -1)
    picked = jnp.einsum("sd,cdr->scr", by_d, fourier, preferred_element_type=jnp.float32)
    by_slot = jnp.sum(jnp.where(in_c[:, :, None], picked, jnp.float32(0.0)), axis=1)
    back = by_slot.astype(jnp.bfloat16).reshape(devices, -1)
    width = back.shape[1]
    padded = -(-width // 256) * 256
    back = jnp.pad(back, ((0, 0), (0, padded - width))).reshape(devices, padded // 128, 128)
    back = lax.all_to_all(back, ("gx", "gy"), 0, 0, tiled=True)
    back = back.reshape(devices, padded)[:, :width].reshape(devices, slot_cap, epoch_count, 2, rows_each)
    returned = jnp.transpose(back, (1, 2, 3, 0, 4)).reshape(slot_cap, epoch_count * 2, lat_rows)
    natural = jnp.einsum(
        "sxr,kr->sxk", returned, onehot, preferred_element_type=jnp.float32
    )
    northern = natural[..., :half_lats]
    southern = natural[..., half_lats:]
    sym_part = ((northern + southern) * weights).astype(jnp.bfloat16)
    anti_part = ((northern - southern) * weights).astype(jnp.bfloat16)
    spectra = analyze(sym_part, anti_part, legendre, orders, epoch_count, 2)
    return (grid_rows, spectra)


def solution(mesh):
    placed = (
        P(("gx", "gy"), None, None, None),
        P(("gx", "gy"), None, None),
        P(("gx", "gy")),
        P(),
        P(),
    )
    return jax.shard_map(
        shards,
        mesh=mesh,
        in_specs=placed,
        out_specs=(P(("gx", "gy"), None, None), P(("gx", "gy"), None, None, None)),
        check_vma=False,
    )
```
